512 devices in a mesh: grp: 16 (over x_hi, y), blk: 32 (over z, x_lo, core).
Axes of the slice: x: 4 (x_hi: 2, x_lo: 2; x = x_hi * 2 + x_lo), y: 8, z: 8, core: 2. Of those that a mesh axis runs over, the one named last changes fastest.
Arguments:
- queries: bfloat16 [512, 8192], P('blk'), may hold values from -6 to 6
- prefix_keys: bfloat16 [65536, 1024], P(('grp', 'blk')), may hold values from -10 to 10
- prefix_values: bfloat16 [65536, 1024], P(('grp', 'blk')), may hold values from -6 to 6
- draft_keys: bfloat16 [512, 1024], P(('grp', 'blk')), may hold values from -12 to 12
- draft_values: bfloat16 [512, 1024], P(('grp', 'blk')), may hold values from -6 to 6
- draft_offset: int32 [512], replicated, may hold values from 0 to 511, as said below
Outputs:
- attended: float32 [512, 8192], P('blk')
The draws below stay inside these ranges and needn't reach their ends.
Inputs may be any that keep to these rules, and one draw needn't show every extreme that they name: Draft token i sees draft keys i - draft_offset[i] through i, and draft_offset[i] <= i.
All inputs are finite; a program needn't handle non-finite values.
Results may differ from the reference program's by a relative error of at most 0.0005.
Values may be sent and summed in bfloat16 or wider, within the bound.
No kernel may reach another device: no remote copies, remote signals or barrier semaphores. Data moves between devices by JAX's collectives and lax.ppermute only.
A program may use at most 128 MiB of HBM per device.

```python
import math
import jax
import jax.numpy as jnp
from jax import lax

H = 64
KV = 8
HD = 128
DRAFT = 512
PREFIX = 65536


def draw_queries(key, part):
    normal = jax.random.normal(jax.random.fold_in(key, 11), (DRAFT, H * HD), jnp.float32)
    values = jnp.clip(normal, -5.0, 5.0)
    return values.astype(jnp.bfloat16)


def draw_prefix_keys(key, part):
    normal = jax.random.normal(jax.random.fold_in(key, 21), (PREFIX, KV * HD), jnp.float32)
    values = jnp.clip(1.5 * normal, -10.0, 10.0)
    return values.astype(jnp.bfloat16)


def draw_draft_offset(key, part):
    position = jnp.arange(DRAFT, dtype=jnp.int32)
    upper_limit = position + 1
    offsets = jax.random.randint(jax.random.fold_in(key, 31), (DRAFT,), 0, upper_limit)
    offsets = offsets.at[DRAFT - 1].set(DRAFT - 1)
    return offsets.astype(jnp.int32)


def level_of(stream_key, extent, split, low, largest):
    gain, own = 1.0, jax.random.fold_in(stream_key, 6)
    for dim, shards_of in split:
        heights = jnp.exp(jax.random.uniform(jax.random.fold_in(own, dim), (shards_of,), jnp.float32, low / len(split), largest / len(split)))
        gain = gain * jnp.repeat(heights, extent[dim] // shards_of).reshape([-1 if axis == dim else 1 for axis in range(len(extent))])
    return gain


def noise(key, dims, deviation, most, pieces=(), kind=jnp.bfloat16):
    loudness = level_of(key, dims, pieces, -0.22, 0.18) if pieces else 1.0
    result = jax.random.normal(key, dims, jnp.float32) * deviation * loudness
    return jnp.minimum(jnp.maximum(result, -most), most).astype(kind)


def setup_inputs(seed: int = 0) -> dict:
    splits = jax.random.split(jax.random.key(seed), 7)
    return {
        "queries": draw_queries(jax.random.fold_in(splits[6], 71), 0),
        "prefix_keys": draw_prefix_keys(jax.random.fold_in(splits[6], 71), 0),
        "prefix_values": noise(splits[2], (PREFIX, KV * HD), 1.0, 6.0, ((0, 512),)),
        "draft_keys": noise(splits[3], (DRAFT, KV * HD), 2.5, 12.0, ((0, 512),)),
        "draft_values": noise(splits[4], (DRAFT, KV * HD), 1.0, 6.0, ((0, 512),)),
        "draft_offset": draw_draft_offset(jax.random.fold_in(splits[6], 71), 0),
    }


def reference(queries, prefix_keys, prefix_values, draft_keys, draft_values, draft_offset):
    group_heads = H // KV
    inverse_root = 1.0 / math.sqrt(HD)
    key_rows = prefix_keys.astype(jnp.float32).reshape(PREFIX, KV, HD)
    value_rows = prefix_values.astype(jnp.float32).reshape(PREFIX, KV, HD)
    draft_key_rows = draft_keys.astype(jnp.float32).reshape(DRAFT, KV, HD)
    draft_value_rows = draft_values.astype(jnp.float32).reshape(DRAFT, KV, HD)
    block_rows = min(16, DRAFT)
    query_blocks = queries.reshape(DRAFT // block_rows, block_rows, KV, group_heads, HD)
    block_starts = jnp.arange(DRAFT // block_rows, dtype=jnp.int32) * block_rows
    key_index = jnp.arange(DRAFT, dtype=jnp.int32)

    def per_block(inputs):
        query_block, block_first = inputs
        query_float = query_block.astype(jnp.float32)
        scores_prefix = jnp.einsum('rkgd,pkd->rkgp', query_float, key_rows, precision=lax.Precision.HIGHEST) * inverse_root
        scores_draft = jnp.einsum('rkgd,pkd->rkgp', query_float, draft_key_rows, precision=lax.Precision.HIGHEST) * inverse_root
        query_index = block_first + jnp.arange(block_rows, dtype=jnp.int32)
        block_offsets = lax.dynamic_slice_in_dim(draft_offset, block_first, block_rows)
        visible = (key_index[None, :] <= query_index[:, None]) & (key_index[None, :] >= (query_index - block_offsets)[:, None])
        visible = visible[:, None, None, :]
        peak = jnp.maximum(lax.optimization_barrier(jnp.max(scores_prefix, axis=3)), lax.optimization_barrier(jnp.max(jnp.where(visible, scores_draft, -jnp.inf), axis=3)))
        weights_prefix = jnp.exp(scores_prefix - peak[..., None])
        weights_draft = jnp.where(visible, jnp.exp(scores_draft - peak[..., None]), 0.0)
        totals = lax.optimization_barrier(jnp.sum(weights_prefix, axis=3)) + lax.optimization_barrier(jnp.sum(weights_draft, axis=3))
        summed = jnp.einsum('rkgp,pkd->rkgd', weights_prefix, value_rows, precision=lax.Precision.HIGHEST)
        summed = summed + jnp.einsum('rkgp,pkd->rkgd', weights_draft, draft_value_rows, precision=lax.Precision.HIGHEST)
        return (summed / totals[..., None]).reshape(block_rows, H * HD)
    attended = lax.map(per_block, (query_blocks, block_starts))
    return attended.reshape(DRAFT, H * HD)
```

```python
import math

import jax
import jax.numpy as jnp
from jax import lax
from jax.sharding import Mesh
from jax.sharding import PartitionSpec as P

H = 64
KV = 8
HD = 128


def split_product(weights, values):
    rounded = lax.reduce_precision(weights, exponent_bits=8, mantissa_bits=7)
    high = rounded.astype(jnp.bfloat16)
    low = (weights - rounded).astype(jnp.bfloat16)
    spec = "rgp,pd->rgd"
    return jnp.einsum(spec, high, values, preferred_element_type=jnp.float32) + jnp.einsum(
        spec, low, values, preferred_element_type=jnp.float32
    )


def local(queries, prefix_keys, prefix_values, draft_keys, draft_values, draft_offset):
    group_heads = H // KV
    rows = queries.shape[0]
    positions = prefix_keys.shape[0]
    ways = lax.axis_size("w")
    quarters = lax.axis_size("zq")
    quarter = lax.axis_index("zq")
    group = lax.axis_index("grp")
    inverse_root = 1.0 / math.sqrt(HD)

    query_heads = queries.reshape(rows, KV, group_heads * HD).transpose(1, 0, 2).reshape(KV, -1)
    key_heads = prefix_keys.reshape(positions, KV, HD).transpose(1, 0, 2).reshape(KV, -1)
    value_heads = prefix_values.reshape(positions, KV, HD).transpose(1, 0, 2).reshape(KV, -1)
    draft_key_heads = draft_keys.reshape(KV, HD)
    draft_value_heads = draft_values.reshape(KV, HD)
    send = jnp.concatenate(
        [query_heads, key_heads, draft_key_heads, value_heads, draft_value_heads], axis=1
    )
    got = lax.all_to_all(send, "w", 0, 0, tiled=True)

    query_size = rows * group_heads * HD
    key_size = positions * HD
    cut = [query_size, key_size, HD, key_size, HD]
    starts = [sum(cut[:n]) for n in range(len(cut))]
    query_block = got[:, : query_size].reshape(ways * rows, group_heads, HD)
    keys_here = jnp.concatenate(
        [
            got[:, starts[1] : starts[1] + key_size].reshape(ways * positions, HD),
            got[:, starts[2] : starts[2] + HD],
        ],
        axis=0,
    )
    values_here = jnp.concatenate(
        [
            got[:, starts[3] : starts[3] + key_size].reshape(ways * positions, HD),
            got[:, starts[4] : starts[4] + HD],
        ],
        axis=0,
    )
    local_keys = ways * positions
    keys_all = lax.all_gather(keys_here, "zq", axis=0)
    values_all = lax.all_gather(values_here, "zq", axis=0)
    prefix_k = keys_all[:, :local_keys].reshape(-1, HD)
    draft_k = keys_all[:, local_keys:].reshape(-1, HD)
    prefix_v = values_all[:, :local_keys].reshape(-1, HD)
    draft_v = values_all[:, local_keys:].reshape(-1, HD)

    block_rows = ways * rows
    scores_prefix = jnp.einsum(
        "rgd,pd->rgp", query_block, prefix_k, preferred_element_type=jnp.float32
    ) * inverse_root
    scores_draft = jnp.einsum(
        "rgd,jd->rgj", query_block, draft_k, preferred_element_type=jnp.float32
    ) * inverse_root

    query_first = quarter * block_rows
    query_index = query_first + lax.iota(jnp.int32, block_rows)
    drafts_per_group = quarters * ways
    key_index = group * drafts_per_group + lax.iota(jnp.int32, drafts_per_group)
    offsets = lax.dynamic_slice_in_dim(draft_offset, query_first, block_rows)
    visible = (key_index[None, :] <= query_index[:, None]) & (
        key_index[None, :] >= (query_index - offsets)[:, None]
    )
    visible = visible[:, None, :]
    masked_draft = jnp.where(visible, scores_draft, -jnp.inf)
    peak = jnp.maximum(jnp.max(scores_prefix, axis=2), jnp.max(masked_draft, axis=2))
    peak = lax.pmax(peak, "grp")

    weights_prefix = jnp.exp(scores_prefix - peak[..., None])
    weights_draft = jnp.where(visible, jnp.exp(masked_draft - peak[..., None]), 0.0)
    totals = jnp.sum(weights_prefix, axis=2) + jnp.sum(weights_draft, axis=2)
    summed = split_product(weights_prefix, prefix_v) + split_product(weights_draft, draft_v)
    summed, totals = lax.psum((summed, totals), "grp")
    attended = summed / totals[..., None]

    attended = attended.reshape(block_rows, 1, group_heads * HD)
    attended = lax.all_to_all(attended, "w", 0, 1, tiled=True)
    return attended.reshape(rows, H * HD)


def solution(mesh):
    groups, blocks = mesh.shape["grp"], mesh.shape["blk"]
    inner = Mesh(mesh.devices.reshape(groups, blocks // KV, KV), ("grp", "zq", "w"))
    rows = ("zq", "w")
    return jax.shard_map(
        local,
        mesh=inner,
        in_specs=(
            P(rows, None),
            P(("grp",) + rows, None),
            P(("grp",) + rows, None),
            P(("grp",) + rows, None),
            P(("grp",) + rows, None),
            P(),
        ),
        out_specs=P(rows, None),
        check_vma=False,
    )
```

```python
import math

import jax
import jax.numpy as jnp
from jax import lax
from jax.sharding import Mesh
from jax.sharding import PartitionSpec as P

H = 64
KV = 8
HD = 128


def split_product(weights, values):
    rounded = lax.reduce_precision(weights, exponent_bits=8, mantissa_bits=7)
    high = rounded.astype(jnp.bfloat16)
    low = (weights - rounded).astype(jnp.bfloat16)
    spec = "rgp,pd->rgd"
    return jnp.einsum(spec, high, values, preferred_element_type=jnp.float32) + jnp.einsum(
        spec, low, values, preferred_element_type=jnp.float32
    )


def local(queries, prefix_keys, prefix_values, draft_keys, draft_values, draft_offset):
    group_heads = H // KV
    rows = queries.shape[0]
    positions = prefix_keys.shape[0]
    ways = lax.axis_size("w")
    quarters = lax.axis_size("zq")
    quarter = lax.axis_index("zq")
    group = lax.axis_index("grp")
    inverse_root = 1.0 / math.sqrt(HD)

    query_heads = queries.reshape(rows, KV, group_heads * HD).transpose(1, 0, 2).reshape(KV, -1)
    key_heads = prefix_keys.reshape(positions, KV, HD).transpose(1, 0, 2).reshape(KV, -1)
    value_heads = prefix_values.reshape(positions, KV, HD).transpose(1, 0, 2).reshape(KV, -1)
    draft_key_heads = draft_keys.reshape(KV, HD)
    draft_value_heads = draft_values.reshape(KV, HD)
    send = jnp.concatenate(
        [query_heads, key_heads, draft_key_heads, value_heads, draft_value_heads], axis=1
    )
    got = lax.all_to_all(send, "w", 0, 0, tiled=True)

    query_size = rows * group_heads * HD
    key_size = positions * HD
    cut = [query_size, key_size, HD, key_size, HD]
    starts = [sum(cut[:n]) for n in range(len(cut))]
    query_block = got[:, : query_size].reshape(ways * rows, group_heads, HD)
    keys_here = jnp.concatenate(
        [
            got[:, starts[1] : starts[1] + key_size].reshape(ways * positions, HD),
            got[:, starts[2] : starts[2] + HD],
        ],
        axis=0,
    )
    values_here = jnp.concatenate(
        [
            got[:, starts[3] : starts[3] + key_size].reshape(ways * positions, HD),
            got[:, starts[4] : starts[4] + HD],
        ],
        axis=0,
    )
    local_keys = ways * positions
    keys_all = lax.all_gather(keys_here, "zq", axis=0)
    values_all = lax.all_gather(values_here, "zq", axis=0)
    prefix_k = keys_all[:, :local_keys].reshape(-1, HD)
    draft_k = keys_all[:, local_keys:].reshape(-1, HD)
    prefix_v = values_all[:, :local_keys].reshape(-1, HD)
    draft_v = values_all[:, local_keys:].reshape(-1, HD)

    block_rows = ways * rows
    scores_prefix = jnp.einsum(
        "rgd,pd->rgp", query_block, prefix_k, preferred_element_type=jnp.float32
    ) * inverse_root
    scores_draft = jnp.einsum(
        "rgd,jd->rgj", query_block, draft_k, preferred_element_type=jnp.float32
    ) * inverse_root

    query_first = quarter * block_rows
    query_index = query_first + lax.iota(jnp.int32, block_rows)
    drafts_per_group = quarters * ways
    key_index = group * drafts_per_group + lax.iota(jnp.int32, drafts_per_group)
    offsets = lax.dynamic_slice_in_dim(draft_offset, query_first, block_rows)
    visible = (key_index[None, :] <= query_index[:, None]) & (
        key_index[None, :] >= (query_index - offsets)[:, None]
    )
    visible = visible[:, None, :]
    masked_draft = jnp.where(visible, scores_draft, -jnp.inf)
    peak = jnp.maximum(jnp.max(scores_prefix, axis=2), jnp.max(masked_draft, axis=2))

    weights_prefix = jnp.exp(scores_prefix - peak[..., None])
    weights_draft = jnp.where(visible, jnp.exp(masked_draft - peak[..., None]), 0.0)
    totals = jnp.sum(weights_prefix, axis=2) + jnp.sum(weights_draft, axis=2)
    summed = split_product(weights_prefix, prefix_v) + split_product(weights_draft, draft_v)

    groups = lax.axis_size("grp")
    slice_rows = block_rows // groups
    packed = jnp.concatenate(
        [
            summed.reshape(groups, -1),
            peak.reshape(groups, -1),
            totals.reshape(groups, -1),
        ],
        axis=1,
    )
    parts = lax.all_to_all(packed, "grp", 0, 0, tiled=True)
    sum_size = slice_rows * group_heads * HD
    head_size = slice_rows * group_heads
    part_sums = parts[:, :sum_size].reshape(groups, slice_rows, group_heads, HD)
    part_peaks = parts[:, sum_size : sum_size + head_size].reshape(groups, slice_rows, group_heads)
    part_totals = parts[:, sum_size + head_size :].reshape(groups, slice_rows, group_heads)
    joined = jnp.max(part_peaks, axis=0)
    scales = jnp.exp(part_peaks - joined[None])
    merged_totals = jnp.sum(part_totals * scales, axis=0)
    merged_sums = jnp.sum(part_sums * scales[..., None], axis=0)
    attended = (merged_sums / merged_totals[..., None]).reshape(slice_rows, group_heads * HD)
    attended = lax.all_gather(attended, "grp", axis=0, tiled=True)

    attended = attended.reshape(block_rows, 1, group_heads * HD)
    attended = lax.all_to_all(attended, "w", 0, 1, tiled=True)
    return attended.reshape(rows, H * HD)


def solution(mesh):
    groups, blocks = mesh.shape["grp"], mesh.shape["blk"]
    inner = Mesh(mesh.devices.reshape(groups, blocks // KV, KV), ("grp", "zq", "w"))
    rows = ("zq", "w")
    return jax.shard_map(
        local,
        mesh=inner,
        in_specs=(
            P(rows, None),
            P(("grp",) + rows, None),
            P(("grp",) + rows, None),
            P(("grp",) + rows, None),
            P(("grp",) + rows, None),
            P(),
        ),
        out_specs=P(rows, None),
        check_vma=False,
    )
```

```python
import math

import jax
import jax.numpy as jnp
from jax import lax
from jax.sharding import Mesh
from jax.sharding import PartitionSpec as P

H = 64
KV = 8
HD = 128


def split_product(weights, values):
    rounded = lax.reduce_precision(weights, exponent_bits=8, mantissa_bits=7)
    high = rounded.astype(jnp.bfloat16)
    low = (weights - rounded).astype(jnp.bfloat16)
    spec = "rgp,pd->rgd"
    return jnp.einsum(spec, high, values, preferred_element_type=jnp.float32) + jnp.einsum(
        spec, low, values, preferred_element_type=jnp.float32
    )


def local(queries, prefix_keys, prefix_values, draft_keys, draft_values, draft_offset):
    group_heads = H // KV
    rows = queries.shape[0]
    positions = prefix_keys.shape[0]
    ways = lax.axis_size("w")
    quarters = lax.axis_size("zq")
    quarter = lax.axis_index("zq")
    group = lax.axis_index("grp")
    inverse_root = 1.0 / math.sqrt(HD)

    query_heads = queries.reshape(rows, KV, group_heads * HD).transpose(1, 0, 2).reshape(KV, -1)
    key_heads = jnp.concatenate(
        [prefix_keys.reshape(positions, KV, HD).transpose(1, 0, 2), draft_keys.reshape(KV, 1, HD)],
        axis=1,
    ).reshape(KV, -1)
    value_heads = jnp.concatenate(
        [prefix_values.reshape(positions, KV, HD).transpose(1, 0, 2), draft_values.reshape(KV, 1, HD)],
        axis=1,
    ).reshape(KV, -1)
    own_quarter = (lax.iota(jnp.int32, quarters) == quarter)[:, None, None]
    query_send = jnp.where(own_quarter, query_heads[None], jnp.zeros_like(query_heads)[None])
    kv_send = jnp.concatenate([key_heads, value_heads], axis=1)
    send = jnp.concatenate(
        [query_send, jnp.broadcast_to(kv_send[None], (quarters,) + kv_send.shape)], axis=2
    ).reshape(quarters * KV, -1)
    got = lax.all_to_all(send, ("zq", "w"), 0, 0, tiled=True)

    query_size = rows * group_heads * HD
    key_size = (positions + 1) * HD
    query_block = lax.dynamic_slice_in_dim(got[:, :query_size], quarter * ways, ways, axis=0)
    query_block = query_block.reshape(ways * rows, group_heads, HD)
    keys_all = got[:, query_size : query_size + key_size].reshape(quarters * ways, positions + 1, HD)
    values_all = got[:, query_size + key_size :].reshape(quarters * ways, positions + 1, HD)
    prefix_k = keys_all[:, :positions].reshape(-1, HD)
    draft_k = keys_all[:, positions]
    prefix_v = values_all[:, :positions].reshape(-1, HD)
    draft_v = values_all[:, positions]

    block_rows = ways * rows
    scores_prefix = jnp.einsum(
        "rgd,pd->rgp", query_block, prefix_k, preferred_element_type=jnp.float32
    ) * inverse_root
    scores_draft = jnp.einsum(
        "rgd,jd->rgj", query_block, draft_k, preferred_element_type=jnp.float32
    ) * inverse_root

    query_first = quarter * block_rows
    query_index = query_first + lax.iota(jnp.int32, block_rows)
    drafts_per_group = quarters * ways
    key_index = group * drafts_per_group + lax.iota(jnp.int32, drafts_per_group)
    offsets = lax.dynamic_slice_in_dim(draft_offset, query_first, block_rows)
    visible = (key_index[None, :] <= query_index[:, None]) & (
        key_index[None, :] >= (query_index - offsets)[:, None]
    )
    visible = visible[:, None, :]
    masked_draft = jnp.where(visible, scores_draft, -jnp.inf)
    peak = jnp.maximum(jnp.max(scores_prefix, axis=2), jnp.max(masked_draft, axis=2))

    weights_prefix = jnp.exp(scores_prefix - peak[..., None])
    weights_draft = jnp.where(visible, jnp.exp(masked_draft - peak[..., None]), 0.0)
    totals = jnp.sum(weights_prefix, axis=2) + jnp.sum(weights_draft, axis=2)
    summed = split_product(weights_prefix, prefix_v) + split_product(weights_draft, draft_v)

    groups = lax.axis_size("grp")
    slice_rows = block_rows // groups
    packed = jnp.concatenate(
        [
            summed.reshape(groups, -1),
            peak.reshape(groups, -1),
            totals.reshape(groups, -1),
        ],
        axis=1,
    )
    parts = lax.all_to_all(packed, "grp", 0, 0, tiled=True)
    sum_size = slice_rows * group_heads * HD
    head_size = slice_rows * group_heads
    part_sums = parts[:, :sum_size].reshape(groups, slice_rows, group_heads, HD)
    part_peaks = parts[:, sum_size : sum_size + head_size].reshape(groups, slice_rows, group_heads)
    part_totals = parts[:, sum_size + head_size :].reshape(groups, slice_rows, group_heads)
    joined = jnp.max(part_peaks, axis=0)
    scales = jnp.exp(part_peaks - joined[None])
    merged_totals = jnp.sum(part_totals * scales, axis=0)
    merged_sums = jnp.sum(part_sums * scales[..., None], axis=0)
    attended = (merged_sums / merged_totals[..., None]).reshape(slice_rows, group_heads * HD)
    attended = jnp.broadcast_to(attended[None], (groups,) + attended.shape)
    attended = lax.all_to_all(attended, "grp", 0, 0, tiled=True)

    attended = attended.reshape(block_rows, 1, group_heads * HD)
    attended = lax.all_to_all(attended, "w", 0, 1, tiled=True)
    return attended.reshape(rows, H * HD)


def solution(mesh):
    groups, blocks = mesh.shape["grp"], mesh.shape["blk"]
    inner = Mesh(mesh.devices.reshape(groups, blocks // KV, KV), ("grp", "zq", "w"))
    rows = ("zq", "w")
    return jax.shard_map(
        local,
        mesh=inner,
        in_specs=(
            P(rows, None),
            P(("grp",) + rows, None),
            P(("grp",) + rows, None),
            P(("grp",) + rows, None),
            P(("grp",) + rows, None),
            P(),
        ),
        out_specs=P(rows, None),
        check_vma=False,
    )
```

```python
import math

import jax
import jax.numpy as jnp
from jax import lax
from jax.sharding import Mesh
from jax.sharding import PartitionSpec as P

H = 64
KV = 8
HD = 128


def split_product(weights, values):
    rounded = lax.reduce_precision(weights, exponent_bits=8, mantissa_bits=7)
    high = rounded.astype(jnp.bfloat16)
    low = (weights - rounded).astype(jnp.bfloat16)
    spec = "rgp,pd->rgd"
    return jnp.einsum(spec, high, values, preferred_element_type=jnp.float32) + jnp.einsum(
        spec, low, values, preferred_element_type=jnp.float32
    )


def local(queries, prefix_keys, prefix_values, draft_keys, draft_values, draft_offset):
    group_heads = H // KV
    rows = queries.shape[0]
    positions = prefix_keys.shape[0]
    ways = lax.axis_size("w")
    quarters = lax.axis_size("zq")
    quarter = lax.axis_index("zq")
    group = lax.axis_index("grp")
    inverse_root = 1.0 / math.sqrt(HD)

    query_heads = queries.reshape(rows, KV, group_heads * HD).transpose(1, 0, 2).reshape(KV, -1)
    key_heads = prefix_keys.reshape(positions, KV, HD).transpose(1, 0, 2).reshape(KV, -1)
    value_heads = prefix_values.reshape(positions, KV, HD).transpose(1, 0, 2).reshape(KV, -1)
    draft_key_heads = draft_keys.reshape(KV, HD)
    draft_value_heads = draft_values.reshape(KV, HD)
    send = jnp.concatenate(
        [query_heads, key_heads, draft_key_heads, value_heads, draft_value_heads], axis=1
    )
    got = lax.all_to_all(send, "w", 0, 0, tiled=True)

    query_size = rows * group_heads * HD
    key_size = positions * HD
    cut = [query_size, key_size, HD, key_size, HD]
    starts = [sum(cut[:n]) for n in range(len(cut))]
    query_block = got[:, : query_size].reshape(ways * rows, group_heads, HD)
    keys_here = jnp.concatenate(
        [
            got[:, starts[1] : starts[1] + key_size].reshape(ways * positions, HD),
            got[:, starts[2] : starts[2] + HD],
        ],
        axis=0,
    )
    values_here = jnp.concatenate(
        [
            got[:, starts[3] : starts[3] + key_size].reshape(ways * positions, HD),
            got[:, starts[4] : starts[4] + HD],
        ],
        axis=0,
    )
    local_keys = ways * positions
    keys_all = lax.all_gather(keys_here, "zq", axis=0)
    values_all = lax.all_gather(values_here, "zq", axis=0)
    prefix_k = keys_all[:, :local_keys].reshape(-1, HD)
    draft_k = keys_all[:, local_keys:].reshape(-1, HD)
    prefix_v = values_all[:, :local_keys].reshape(-1, HD)
    draft_v = values_all[:, local_keys:].reshape(-1, HD)

    block_rows = ways * rows
    scores_prefix = jnp.einsum(
        "rgd,pd->rgp", query_block, prefix_k, preferred_element_type=jnp.float32
    ) * inverse_root
    scores_draft = jnp.einsum(
        "rgd,jd->rgj", query_block, draft_k, preferred_element_type=jnp.float32
    ) * inverse_root

    query_first = quarter * block_rows
    query_index = query_first + lax.iota(jnp.int32, block_rows)
    drafts_per_group = quarters * ways
    key_index = group * drafts_per_group + lax.iota(jnp.int32, drafts_per_group)
    offsets = lax.dynamic_slice_in_dim(draft_offset, query_first, block_rows)
    visible = (key_index[None, :] <= query_index[:, None]) & (
        key_index[None, :] >= (query_index - offsets)[:, None]
    )
    visible = visible[:, None, :]
    masked_draft = jnp.where(visible, scores_draft, -jnp.inf)
    peak = jnp.maximum(jnp.max(scores_prefix, axis=2), jnp.max(masked_draft, axis=2))

    weights_prefix = jnp.exp(scores_prefix - peak[..., None])
    weights_draft = jnp.where(visible, jnp.exp(masked_draft - peak[..., None]), 0.0)
    totals = jnp.sum(weights_prefix, axis=2) + jnp.sum(weights_draft, axis=2)
    summed = split_product(weights_prefix, prefix_v) + split_product(weights_draft, draft_v)

    groups = lax.axis_size("grp")
    slice_rows = block_rows // groups
    packed = jnp.concatenate(
        [
            summed.reshape(groups, -1),
            peak.reshape(groups, -1),
            totals.reshape(groups, -1),
        ],
        axis=1,
    )
    parts = lax.all_to_all(packed, "grp", 0, 0, tiled=True)
    sum_size = slice_rows * group_heads * HD
    head_size = slice_rows * group_heads
    part_sums = parts[:, :sum_size].reshape(groups, slice_rows, group_heads, HD)
    part_peaks = parts[:, sum_size : sum_size + head_size].reshape(groups, slice_rows, group_heads)
    part_totals = parts[:, sum_size + head_size :].reshape(groups, slice_rows, group_heads)
    joined = jnp.max(part_peaks, axis=0)
    scales = jnp.exp(part_peaks - joined[None])
    merged_totals = jnp.sum(part_totals * scales, axis=0)
    merged_sums = jnp.sum(part_sums * scales[..., None], axis=0)
    attended = (merged_sums / merged_totals[..., None]).reshape(slice_rows, group_heads * HD)
    attended = jnp.broadcast_to(attended[None], (groups,) + attended.shape)
    attended = lax.all_to_all(attended, "grp", 0, 0, tiled=True)

    attended = attended.reshape(block_rows, 1, group_heads * HD)
    attended = lax.all_to_all(attended, "w", 0, 1, tiled=True)
    return attended.reshape(rows, H * HD)


def solution(mesh):
    groups, blocks = mesh.shape["grp"], mesh.shape["blk"]
    inner = Mesh(mesh.devices.reshape(groups, blocks // KV, KV), ("grp", "zq", "w"))
    rows = ("zq", "w")
    return jax.shard_map(
        local,
        mesh=inner,
        in_specs=(
            P(rows, None),
            P(("grp",) + rows, None),
            P(("grp",) + rows, None),
            P(("grp",) + rows, None),
            P(("grp",) + rows, None),
            P(),
        ),
        out_specs=P(rows, None),
        check_vma=False,
    )
```

```python
import math

import jax
import jax.numpy as jnp
from jax import lax
from jax.sharding import Mesh
from jax.sharding import PartitionSpec as P

H = 64
KV = 8
HD = 128


def split_product(weights, values):
    rounded = lax.reduce_precision(weights, exponent_bits=8, mantissa_bits=7)
    high = rounded.astype(jnp.bfloat16)
    low = (weights - rounded).astype(jnp.bfloat16)
    spec = "rgp,pd->rgd"
    return jnp.einsum(spec, high, values, preferred_element_type=jnp.float32) + jnp.einsum(
        spec, low, values, preferred_element_type=jnp.float32
    )


def local(queries, prefix_keys, prefix_values, draft_keys, draft_values, draft_offset):
    group_heads = H // KV
    rows = queries.shape[0]
    positions = prefix_keys.shape[0]
    ways = lax.axis_size("w")
    quarters = lax.axis_size("zq")
    quarter = lax.axis_index("zq")
    group = lax.axis_index("grp")
    inverse_root = 1.0 / math.sqrt(HD)

    query_heads = queries.reshape(rows, KV, group_heads * HD).transpose(1, 0, 2).reshape(KV, -1)
    key_heads = prefix_keys.reshape(positions, KV, HD).transpose(1, 0, 2).reshape(KV, -1)
    value_heads = prefix_values.reshape(positions, KV, HD).transpose(1, 0, 2).reshape(KV, -1)
    draft_key_heads = draft_keys.reshape(KV, HD)
    draft_value_heads = draft_values.reshape(KV, HD)
    send = jnp.concatenate(
        [query_heads, key_heads, draft_key_heads, value_heads, draft_value_heads], axis=1
    )
    got = lax.all_to_all(send, "w", 0, 0, tiled=True)

    query_size = rows * group_heads * HD
    key_size = positions * HD
    cut = [query_size, key_size, HD, key_size, HD]
    starts = [sum(cut[:n]) for n in range(len(cut))]
    query_block = got[:, : query_size].reshape(ways * rows, group_heads, HD)
    keys_here = jnp.concatenate(
        [
            got[:, starts[1] : starts[1] + key_size].reshape(ways * positions, HD),
            got[:, starts[2] : starts[2] + HD],
        ],
        axis=0,
    )
    values_here = jnp.concatenate(
        [
            got[:, starts[3] : starts[3] + key_size].reshape(ways * positions, HD),
            got[:, starts[4] : starts[4] + HD],
        ],
        axis=0,
    )
    local_keys = ways * positions
    both_all = lax.all_gather(jnp.stack([keys_here, values_here]), "zq", axis=0)
    keys_all, values_all = both_all[:, 0], both_all[:, 1]
    prefix_k = keys_all[:, :local_keys].reshape(-1, HD)
    draft_k = keys_all[:, local_keys:].reshape(-1, HD)
    prefix_v = values_all[:, :local_keys].reshape(-1, HD)
    draft_v = values_all[:, local_keys:].reshape(-1, HD)

    block_rows = ways * rows
    scores_prefix = jnp.einsum(
        "rgd,pd->rgp", query_block, prefix_k, preferred_element_type=jnp.float32
    ) * inverse_root
    scores_draft = jnp.einsum(
        "rgd,jd->rgj", query_block, draft_k, preferred_element_type=jnp.float32
    ) * inverse_root

    query_first = quarter * block_rows
    query_index = query_first + lax.iota(jnp.int32, block_rows)
    drafts_per_group = quarters * ways
    key_index = group * drafts_per_group + lax.iota(jnp.int32, drafts_per_group)
    offsets = lax.dynamic_slice_in_dim(draft_offset, query_first, block_rows)
    visible = (key_index[None, :] <= query_index[:, None]) & (
        key_index[None, :] >= (query_index - offsets)[:, None]
    )
    visible = visible[:, None, :]
    masked_draft = jnp.where(visible, scores_draft, -jnp.inf)
    peak = jnp.maximum(jnp.max(scores_prefix, axis=2), jnp.max(masked_draft, axis=2))

    weights_prefix = jnp.exp(scores_prefix - peak[..., None])
    weights_draft = jnp.where(visible, jnp.exp(masked_draft - peak[..., None]), 0.0)
    totals = jnp.sum(weights_prefix, axis=2) + jnp.sum(weights_draft, axis=2)
    summed = split_product(weights_prefix, prefix_v) + split_product(weights_draft, draft_v)

    groups = lax.axis_size("grp")
    slice_rows = block_rows // groups
    packed = jnp.concatenate(
        [
            summed.reshape(groups, -1),
            peak.reshape(groups, -1),
            totals.reshape(groups, -1),
        ],
        axis=1,
    )
    parts = lax.all_to_all(packed, "grp", 0, 0, tiled=True)
    sum_size = slice_rows * group_heads * HD
    head_size = slice_rows * group_heads
    part_sums = parts[:, :sum_size].reshape(groups, slice_rows, group_heads, HD)
    part_peaks = parts[:, sum_size : sum_size + head_size].reshape(groups, slice_rows, group_heads)
    part_totals = parts[:, sum_size + head_size :].reshape(groups, slice_rows, group_heads)
    joined = jnp.max(part_peaks, axis=0)
    scales = jnp.exp(part_peaks - joined[None])
    merged_totals = jnp.sum(part_totals * scales, axis=0)
    merged_sums = jnp.sum(part_sums * scales[..., None], axis=0)
    attended = (merged_sums / merged_totals[..., None]).reshape(slice_rows, group_heads * HD)
    attended = jnp.broadcast_to(attended[None], (groups,) + attended.shape)
    attended = lax.all_to_all(attended, "grp", 0, 0, tiled=True)

    attended = attended.reshape(block_rows, 1, group_heads * HD)
    attended = lax.all_to_all(attended, "w", 0, 1, tiled=True)
    return attended.reshape(rows, H * HD)


def solution(mesh):
    groups, blocks = mesh.shape["grp"], mesh.shape["blk"]
    inner = Mesh(mesh.devices.reshape(groups, blocks // KV, KV), ("grp", "zq", "w"))
    rows = ("zq", "w")
    return jax.shard_map(
        local,
        mesh=inner,
        in_specs=(
            P(rows, None),
            P(("grp",) + rows, None),
            P(("grp",) + rows, None),
            P(("grp",) + rows, None),
            P(("grp",) + rows, None),
            P(),
        ),
        out_specs=P(rows, None),
        check_vma=False,
    )
```

```python
import functools
import math

import jax
import jax.numpy as jnp
from jax import lax
from jax.experimental import pallas as pl
from jax.experimental.pallas import tpu as pltpu
from jax.sharding import Mesh
from jax.sharding import PartitionSpec as P

H = 64
KV = 8
HD = 128


def split_product(weights, values):
    rounded = lax.reduce_precision(weights, exponent_bits=8, mantissa_bits=7)
    high = rounded.astype(jnp.bfloat16)
    low = (weights - rounded).astype(jnp.bfloat16)
    spec = "rgp,pd->rgd"
    return jnp.einsum(spec, high, values, preferred_element_type=jnp.float32) + jnp.einsum(
        spec, low, values, preferred_element_type=jnp.float32
    )


def attend_kernel(inverse_root, query_ref, key_ref, value_ref, sum_ref, peak_ref, total_ref):
    scores = lax.dot_general(
        query_ref[...],
        key_ref[...],
        (((1,), (1,)), ((), ())),
        preferred_element_type=jnp.float32,
    ) * inverse_root
    peak = jnp.max(scores, axis=1, keepdims=True)
    weights = jnp.exp(scores - peak)
    total_ref[...] = jnp.sum(weights, axis=1, keepdims=True)
    peak_ref[...] = peak
    high = weights.astype(jnp.bfloat16)
    low = (weights - high.astype(jnp.float32)).astype(jnp.bfloat16)
    values = value_ref[...]
    sum_ref[...] = jnp.dot(high, values, preferred_element_type=jnp.float32) + jnp.dot(
        low, values, preferred_element_type=jnp.float32
    )


def attend_prefix(query_rows, keys, values, inverse_root):
    count, width = query_rows.shape
    length = keys.shape[0]
    tile = 256
    return pl.pallas_call(
        functools.partial(attend_kernel, inverse_root),
        grid=(count // tile,),
        in_specs=[
            pl.BlockSpec((tile, width), lambda i: (i, 0)),
            pl.BlockSpec((length, width), lambda i: (0, 0)),
            pl.BlockSpec((length, width), lambda i: (0, 0)),
        ],
        out_specs=[
            pl.BlockSpec((tile, width), lambda i: (i, 0)),
            pl.BlockSpec((tile, 1), lambda i: (i, 0)),
            pl.BlockSpec((tile, 1), lambda i: (i, 0)),
        ],
        out_shape=[
            jax.ShapeDtypeStruct((count, width), jnp.float32),
            jax.ShapeDtypeStruct((count, 1), jnp.float32),
            jax.ShapeDtypeStruct((count, 1), jnp.float32),
        ],
        compiler_params=pltpu.CompilerParams(vmem_limit_bytes=48 * 1024 * 1024),
        cost_estimate=pl.CostEstimate(
            flops=6 * count * length * width,
            transcendentals=count * length,
            bytes_accessed=2 * count * width + 4 * length * width + 4 * count * (width + 2),
        ),
    )(query_rows, keys, values)


def local(queries, prefix_keys, prefix_values, draft_keys, draft_values, draft_offset):
    group_heads = H // KV
    rows = queries.shape[0]
    positions = prefix_keys.shape[0]
    ways = lax.axis_size("w")
    quarters = lax.axis_size("zq")
    quarter = lax.axis_index("zq")
    group = lax.axis_index("grp")
    inverse_root = 1.0 / math.sqrt(HD)

    query_heads = queries.reshape(rows, KV, group_heads * HD).transpose(1, 0, 2).reshape(KV, -1)
    key_heads = prefix_keys.reshape(positions, KV, HD).transpose(1, 0, 2).reshape(KV, -1)
    value_heads = prefix_values.reshape(positions, KV, HD).transpose(1, 0, 2).reshape(KV, -1)
    draft_key_heads = draft_keys.reshape(KV, HD)
    draft_value_heads = draft_values.reshape(KV, HD)
    send = jnp.concatenate(
        [query_heads, key_heads, draft_key_heads, value_heads, draft_value_heads], axis=1
    )
    got = lax.all_to_all(send, "w", 0, 0, tiled=True)

    query_size = rows * group_heads * HD
    key_size = positions * HD
    cut = [query_size, key_size, HD, key_size, HD]
    starts = [sum(cut[:n]) for n in range(len(cut))]
    query_block = got[:, : query_size].reshape(ways * rows, group_heads, HD)
    keys_here = jnp.concatenate(
        [
            got[:, starts[1] : starts[1] + key_size].reshape(ways * positions, HD),
            got[:, starts[2] : starts[2] + HD],
        ],
        axis=0,
    )
    values_here = jnp.concatenate(
        [
            got[:, starts[3] : starts[3] + key_size].reshape(ways * positions, HD),
            got[:, starts[4] : starts[4] + HD],
        ],
        axis=0,
    )
    local_keys = ways * positions
    both_all = lax.all_gather(jnp.stack([keys_here, values_here]), "zq", axis=0)
    keys_all, values_all = both_all[:, 0], both_all[:, 1]
    prefix_k = keys_all[:, :local_keys].reshape(-1, HD)
    draft_k = keys_all[:, local_keys:].reshape(-1, HD)
    prefix_v = values_all[:, :local_keys].reshape(-1, HD)
    draft_v = values_all[:, local_keys:].reshape(-1, HD)

    block_rows = ways * rows
    query_rows = query_block.reshape(block_rows * group_heads, HD)
    prefix_sum, prefix_peak, prefix_total = attend_prefix(query_rows, prefix_k, prefix_v, inverse_root)
    prefix_sum = prefix_sum.reshape(block_rows, group_heads, HD)
    prefix_peak = prefix_peak.reshape(block_rows, group_heads)
    prefix_total = prefix_total.reshape(block_rows, group_heads)
    scores_draft = jnp.einsum(
        "rgd,jd->rgj", query_block, draft_k, preferred_element_type=jnp.float32
    ) * inverse_root

    query_first = quarter * block_rows
    query_index = query_first + lax.iota(jnp.int32, block_rows)
    drafts_per_group = quarters * ways
    key_index = group * drafts_per_group + lax.iota(jnp.int32, drafts_per_group)
    offsets = lax.dynamic_slice_in_dim(draft_offset, query_first, block_rows)
    visible = (key_index[None, :] <= query_index[:, None]) & (
        key_index[None, :] >= (query_index - offsets)[:, None]
    )
    visible = visible[:, None, :]
    masked_draft = jnp.where(visible, scores_draft, -jnp.inf)
    peak = jnp.maximum(prefix_peak, jnp.max(masked_draft, axis=2))
    prefix_scale = jnp.exp(prefix_peak - peak)
    weights_draft = jnp.where(visible, jnp.exp(masked_draft - peak[..., None]), 0.0)
    totals = prefix_total * prefix_scale + jnp.sum(weights_draft, axis=2)
    summed = prefix_sum * prefix_scale[..., None] + split_product(weights_draft, draft_v)

    groups = lax.axis_size("grp")
    slice_rows = block_rows // groups
    packed = jnp.concatenate(
        [
            summed.reshape(groups, -1),
            peak.reshape(groups, -1),
            totals.reshape(groups, -1),
        ],
        axis=1,
    )
    parts = lax.all_to_all(packed, "grp", 0, 0, tiled=True)
    sum_size = slice_rows * group_heads * HD
    head_size = slice_rows * group_heads
    part_sums = parts[:, :sum_size].reshape(groups, slice_rows, group_heads, HD)
    part_peaks = parts[:, sum_size : sum_size + head_size].reshape(groups, slice_rows, group_heads)
    part_totals = parts[:, sum_size + head_size :].reshape(groups, slice_rows, group_heads)
    joined = jnp.max(part_peaks, axis=0)
    scales = jnp.exp(part_peaks - joined[None])
    merged_totals = jnp.sum(part_totals * scales, axis=0)
    merged_sums = jnp.sum(part_sums * scales[..., None], axis=0)
    attended = (merged_sums / merged_totals[..., None]).reshape(slice_rows, group_heads * HD)
    attended = jnp.broadcast_to(attended[None], (groups,) + attended.shape)
    attended = lax.all_to_all(attended, "grp", 0, 0, tiled=True)

    attended = attended.reshape(block_rows, 1, group_heads * HD)
    attended = lax.all_to_all(attended, "w", 0, 1, tiled=True)
    return attended.reshape(rows, H * HD)


def solution(mesh):
    groups, blocks = mesh.shape["grp"], mesh.shape["blk"]
    inner = Mesh(mesh.devices.reshape(groups, blocks // KV, KV), ("grp", "zq", "w"))
    rows = ("zq", "w")
    return jax.shard_map(
        local,
        mesh=inner,
        in_specs=(
            P(rows, None),
            P(("grp",) + rows, None),
            P(("grp",) + rows, None),
            P(("grp",) + rows, None),
            P(("grp",) + rows, None),
            P(),
        ),
        out_specs=P(rows, None),
        check_vma=False,
    )
```

```python
import functools
import math

import jax
import jax.numpy as jnp
from jax import lax
from jax.experimental import pallas as pl
from jax.experimental.pallas import tpu as pltpu
from jax.sharding import Mesh
from jax.sharding import PartitionSpec as P

H = 64
KV = 8
HD = 128


def split_product(weights, values):
    rounded = lax.reduce_precision(weights, exponent_bits=8, mantissa_bits=7)
    high = rounded.astype(jnp.bfloat16)
    low = (weights - rounded).astype(jnp.bfloat16)
    spec = "rgp,pd->rgd"
    return jnp.einsum(spec, high, values, preferred_element_type=jnp.float32) + jnp.einsum(
        spec, low, values, preferred_element_type=jnp.float32
    )


def attend_kernel(inverse_root, query_ref, key_ref, value_ref, sum_ref, peak_ref, total_ref):
    scores = lax.dot_general(
        query_ref[...],
        key_ref[...],
        (((1,), (1,)), ((), ())),
        preferred_element_type=jnp.float32,
    ) * inverse_root
    peak = jnp.max(scores, axis=1, keepdims=True)
    weights = jnp.exp(scores - peak)
    total_ref[...] = jnp.sum(weights, axis=1, keepdims=True)
    peak_ref[...] = peak
    high = weights.astype(jnp.bfloat16)
    low = (weights - high.astype(jnp.float32)).astype(jnp.bfloat16)
    values = value_ref[...]
    sum_ref[...] = jnp.dot(high, values, preferred_element_type=jnp.float32) + jnp.dot(
        low, values, preferred_element_type=jnp.float32
    )


def attend_prefix(query_rows, keys, values, inverse_root):
    count, width = query_rows.shape
    length = keys.shape[0]
    tile = 256
    return pl.pallas_call(
        functools.partial(attend_kernel, inverse_root),
        grid=(count // tile,),
        in_specs=[
            pl.BlockSpec((tile, width), lambda i: (i, 0)),
            pl.BlockSpec((length, width), lambda i: (0, 0)),
            pl.BlockSpec((length, width), lambda i: (0, 0)),
        ],
        out_specs=[
            pl.BlockSpec((tile, width), lambda i: (i, 0)),
            pl.BlockSpec((tile, 1), lambda i: (i, 0)),
            pl.BlockSpec((tile, 1), lambda i: (i, 0)),
        ],
        out_shape=[
            jax.ShapeDtypeStruct((count, width), jnp.float32),
            jax.ShapeDtypeStruct((count, 1), jnp.float32),
            jax.ShapeDtypeStruct((count, 1), jnp.float32),
        ],
        compiler_params=pltpu.CompilerParams(vmem_limit_bytes=48 * 1024 * 1024),
        cost_estimate=pl.CostEstimate(
            flops=6 * count * length * width,
            transcendentals=count * length,
            bytes_accessed=2 * count * width + 4 * length * width + 4 * count * (width + 2),
        ),
    )(query_rows, keys, values)


def local(queries, prefix_keys, prefix_values, draft_keys, draft_values, draft_offset):
    group_heads = H // KV
    rows = queries.shape[0]
    positions = prefix_keys.shape[0]
    ways = lax.axis_size("w")
    quarters = lax.axis_size("zq")
    quarter = lax.axis_index("zq")
    group = lax.axis_index("grp")
    inverse_root = 1.0 / math.sqrt(HD)

    query_heads = queries.reshape(rows, KV, group_heads * HD).transpose(1, 0, 2).reshape(KV, -1)
    key_heads = prefix_keys.reshape(positions, KV, HD).transpose(1, 0, 2).reshape(KV, -1)
    value_heads = prefix_values.reshape(positions, KV, HD).transpose(1, 0, 2).reshape(KV, -1)
    draft_key_heads = draft_keys.reshape(KV, HD)
    draft_value_heads = draft_values.reshape(KV, HD)
    send = jnp.concatenate(
        [query_heads, key_heads, draft_key_heads, value_heads, draft_value_heads], axis=1
    )
    got = lax.all_to_all(send, "w", 0, 0, tiled=True)

    query_size = rows * group_heads * HD
    key_size = positions * HD
    cut = [query_size, key_size, HD, key_size, HD]
    starts = [sum(cut[:n]) for n in range(len(cut))]
    query_block = got[:, : query_size].reshape(ways * rows, group_heads, HD)
    keys_here = jnp.concatenate(
        [
            got[:, starts[1] : starts[1] + key_size].reshape(ways * positions, HD),
            got[:, starts[2] : starts[2] + HD],
        ],
        axis=0,
    )
    values_here = jnp.concatenate(
        [
            got[:, starts[3] : starts[3] + key_size].reshape(ways * positions, HD),
            got[:, starts[4] : starts[4] + HD],
        ],
        axis=0,
    )
    local_keys = ways * positions
    both_here = jnp.stack([keys_here, values_here])
    blocks = [both_here] + [
        lax.ppermute(both_here, "zq", [(i, (i + shift) % quarters) for i in range(quarters)])
        for shift in range(1, quarters)
    ]
    both_all = jnp.stack(blocks)
    keys_all, values_all = both_all[:, 0], both_all[:, 1]
    prefix_k = keys_all[:, :local_keys].reshape(-1, HD)
    draft_k = keys_all[:, local_keys:].reshape(-1, HD)
    prefix_v = values_all[:, :local_keys].reshape(-1, HD)
    draft_v = values_all[:, local_keys:].reshape(-1, HD)
    source_quarter = (quarter - lax.iota(jnp.int32, quarters)) % quarters

    block_rows = ways * rows
    query_rows = query_block.reshape(block_rows * group_heads, HD)
    prefix_sum, prefix_peak, prefix_total = attend_prefix(query_rows, prefix_k, prefix_v, inverse_root)
    prefix_sum = prefix_sum.reshape(block_rows, group_heads, HD)
    prefix_peak = prefix_peak.reshape(block_rows, group_heads)
    prefix_total = prefix_total.reshape(block_rows, group_heads)
    scores_draft = jnp.einsum(
        "rgd,jd->rgj", query_block, draft_k, preferred_element_type=jnp.float32
    ) * inverse_root

    query_first = quarter * block_rows
    query_index = query_first + lax.iota(jnp.int32, block_rows)
    drafts_per_group = quarters * ways
    draft_source = (source_quarter[:, None] * ways + lax.iota(jnp.int32, ways)[None, :]).reshape(-1)
    key_index = group * drafts_per_group + draft_source
    offsets = lax.dynamic_slice_in_dim(draft_offset, query_first, block_rows)
    visible = (key_index[None, :] <= query_index[:, None]) & (
        key_index[None, :] >= (query_index - offsets)[:, None]
    )
    visible = visible[:, None, :]
    masked_draft = jnp.where(visible, scores_draft, -jnp.inf)
    peak = jnp.maximum(prefix_peak, jnp.max(masked_draft, axis=2))
    prefix_scale = jnp.exp(prefix_peak - peak)
    weights_draft = jnp.where(visible, jnp.exp(masked_draft - peak[..., None]), 0.0)
    totals = prefix_total * prefix_scale + jnp.sum(weights_draft, axis=2)
    summed = prefix_sum * prefix_scale[..., None] + split_product(weights_draft, draft_v)

    groups = lax.axis_size("grp")
    slice_rows = block_rows // groups
    packed = jnp.concatenate(
        [
            summed.reshape(groups, -1),
            peak.reshape(groups, -1),
            totals.reshape(groups, -1),
        ],
        axis=1,
    )
    parts = lax.all_to_all(packed, "grp", 0, 0, tiled=True)
    sum_size = slice_rows * group_heads * HD
    head_size = slice_rows * group_heads
    part_sums = parts[:, :sum_size].reshape(groups, slice_rows, group_heads, HD)
    part_peaks = parts[:, sum_size : sum_size + head_size].reshape(groups, slice_rows, group_heads)
    part_totals = parts[:, sum_size + head_size :].reshape(groups, slice_rows, group_heads)
    joined = jnp.max(part_peaks, axis=0)
    scales = jnp.exp(part_peaks - joined[None])
    merged_totals = jnp.sum(part_totals * scales, axis=0)
    merged_sums = jnp.sum(part_sums * scales[..., None], axis=0)
    attended = (merged_sums / merged_totals[..., None]).reshape(slice_rows, group_heads * HD)
    attended = jnp.broadcast_to(attended[None], (groups,) + attended.shape)
    attended = lax.all_to_all(attended, "grp", 0, 0, tiled=True)

    attended = attended.reshape(block_rows, 1, group_heads * HD)
    attended = lax.all_to_all(attended, "w", 0, 1, tiled=True)
    return attended.reshape(rows, H * HD)


def solution(mesh):
    groups, blocks = mesh.shape["grp"], mesh.shape["blk"]
    inner = Mesh(mesh.devices.reshape(groups, blocks // KV, KV), ("grp", "zq", "w"))
    rows = ("zq", "w")
    return jax.shard_map(
        local,
        mesh=inner,
        in_specs=(
            P(rows, None),
            P(("grp",) + rows, None),
            P(("grp",) + rows, None),
            P(("grp",) + rows, None),
            P(("grp",) + rows, None),
            P(),
        ),
        out_specs=P(rows, None),
        check_vma=False,
    )
```

```python
import functools
import math

import jax
import jax.numpy as jnp
from jax import lax
from jax.experimental import pallas as pl
from jax.experimental.pallas import tpu as pltpu
from jax.sharding import Mesh
from jax.sharding import PartitionSpec as P

H = 64
KV = 8
HD = 128


def split_product(weights, values):
    rounded = lax.reduce_precision(weights, exponent_bits=8, mantissa_bits=7)
    high = rounded.astype(jnp.bfloat16)
    low = (weights - rounded).astype(jnp.bfloat16)
    spec = "rgp,pd->rgd"
    return jnp.einsum(spec, high, values, preferred_element_type=jnp.float32) + jnp.einsum(
        spec, low, values, preferred_element_type=jnp.float32
    )


def attend_kernel(inverse_root, query_ref, key_ref, value_ref, sum_ref, peak_ref, total_ref):
    scores = lax.dot_general(
        query_ref[...],
        key_ref[...],
        (((1,), (1,)), ((), ())),
        preferred_element_type=jnp.float32,
    ) * inverse_root
    peak = jnp.max(scores, axis=1, keepdims=True)
    weights = jnp.exp(scores - peak)
    total_ref[...] = jnp.sum(weights, axis=1, keepdims=True)
    peak_ref[...] = peak
    high = weights.astype(jnp.bfloat16)
    low = (weights - high.astype(jnp.float32)).astype(jnp.bfloat16)
    values = value_ref[...]
    sum_ref[...] = jnp.dot(high, values, preferred_element_type=jnp.float32) + jnp.dot(
        low, values, preferred_element_type=jnp.float32
    )


def attend_prefix(query_rows, keys, values, inverse_root):
    count, width = query_rows.shape
    length = keys.shape[0]
    tile = 256
    return pl.pallas_call(
        functools.partial(attend_kernel, inverse_root),
        grid=(count // tile,),
        in_specs=[
            pl.BlockSpec((tile, width), lambda i: (i, 0)),
            pl.BlockSpec((length, width), lambda i: (0, 0)),
            pl.BlockSpec((length, width), lambda i: (0, 0)),
        ],
        out_specs=[
            pl.BlockSpec((tile, width), lambda i: (i, 0)),
            pl.BlockSpec((tile, 1), lambda i: (i, 0)),
            pl.BlockSpec((tile, 1), lambda i: (i, 0)),
        ],
        out_shape=[
            jax.ShapeDtypeStruct((count, width), jnp.float32),
            jax.ShapeDtypeStruct((count, 1), jnp.float32),
            jax.ShapeDtypeStruct((count, 1), jnp.float32),
        ],
        compiler_params=pltpu.CompilerParams(vmem_limit_bytes=48 * 1024 * 1024),
        cost_estimate=pl.CostEstimate(
            flops=6 * count * length * width,
            transcendentals=count * length,
            bytes_accessed=2 * count * width + 4 * length * width + 4 * count * (width + 2),
        ),
    )(query_rows, keys, values)


def local(queries, prefix_keys, prefix_values, draft_keys, draft_values, draft_offset):
    group_heads = H // KV
    rows = queries.shape[0]
    positions = prefix_keys.shape[0]
    ways = lax.axis_size("w")
    quarters = lax.axis_size("zq")
    quarter = lax.axis_index("zq")
    group = lax.axis_index("grp")
    inverse_root = 1.0 / math.sqrt(HD)

    query_heads = queries.reshape(rows, KV, group_heads * HD).transpose(1, 0, 2).reshape(KV, -1)
    key_heads = prefix_keys.reshape(positions, KV, HD).transpose(1, 0, 2).reshape(KV, -1)
    value_heads = prefix_values.reshape(positions, KV, HD).transpose(1, 0, 2).reshape(KV, -1)
    draft_key_heads = draft_keys.reshape(KV, HD)
    draft_value_heads = draft_values.reshape(KV, HD)
    send = jnp.concatenate(
        [query_heads, key_heads, draft_key_heads, value_heads, draft_value_heads], axis=1
    )
    got = lax.all_to_all(send, "w", 0, 0, tiled=True)

    query_size = rows * group_heads * HD
    key_size = positions * HD
    cut = [query_size, key_size, HD, key_size, HD]
    starts = [sum(cut[:n]) for n in range(len(cut))]
    query_block = got[:, : query_size].reshape(ways * rows, group_heads, HD)
    keys_here = jnp.concatenate(
        [
            got[:, starts[1] : starts[1] + key_size].reshape(ways * positions, HD),
            got[:, starts[2] : starts[2] + HD],
        ],
        axis=0,
    )
    values_here = jnp.concatenate(
        [
            got[:, starts[3] : starts[3] + key_size].reshape(ways * positions, HD),
            got[:, starts[4] : starts[4] + HD],
        ],
        axis=0,
    )
    local_keys = ways * positions
    both_here = jnp.stack([keys_here, values_here])
    blocks = [both_here] + [
        lax.ppermute(both_here, "zq", [(i, (i + shift) % quarters) for i in range(quarters)])
        for shift in range(1, quarters)
    ]
    both_all = jnp.stack(blocks)
    keys_all, values_all = both_all[:, 0], both_all[:, 1]
    prefix_k = keys_all[:, :local_keys].reshape(-1, HD)
    draft_k = keys_all[:, local_keys:].reshape(-1, HD)
    prefix_v = values_all[:, :local_keys].reshape(-1, HD)
    draft_v = values_all[:, local_keys:].reshape(-1, HD)
    source_quarter = (quarter - lax.iota(jnp.int32, quarters)) % quarters

    block_rows = ways * rows
    query_rows = query_block.reshape(block_rows * group_heads, HD)
    prefix_sum, prefix_peak, prefix_total = attend_prefix(query_rows, prefix_k, prefix_v, inverse_root)
    prefix_sum = prefix_sum.reshape(block_rows, group_heads, HD)
    prefix_peak = prefix_peak.reshape(block_rows, group_heads)
    prefix_total = prefix_total.reshape(block_rows, group_heads)
    scores_draft = jnp.einsum(
        "rgd,jd->rgj", query_block, draft_k, preferred_element_type=jnp.float32
    ) * inverse_root

    query_first = quarter * block_rows
    query_index = query_first + lax.iota(jnp.int32, block_rows)
    drafts_per_group = quarters * ways
    draft_source = (source_quarter[:, None] * ways + lax.iota(jnp.int32, ways)[None, :]).reshape(-1)
    key_index = group * drafts_per_group + draft_source
    offsets = lax.dynamic_slice_in_dim(draft_offset, query_first, block_rows)
    visible = (key_index[None, :] <= query_index[:, None]) & (
        key_index[None, :] >= (query_index - offsets)[:, None]
    )
    visible = visible[:, None, :]
    masked_draft = jnp.where(visible, scores_draft, -jnp.inf)
    peak = jnp.maximum(prefix_peak, jnp.max(masked_draft, axis=2))
    prefix_scale = jnp.exp(prefix_peak - peak)
    weights_draft = jnp.where(visible, jnp.exp(masked_draft - peak[..., None]), 0.0)
    totals = prefix_total * prefix_scale + jnp.sum(weights_draft, axis=2)
    summed = prefix_sum * prefix_scale[..., None] + split_product(weights_draft, draft_v)

    groups = lax.axis_size("grp")
    def by_destination(part):
        part = part.reshape((ways, groups) + part.shape[1:])
        return part.transpose((1, 0) + tuple(range(2, part.ndim))).reshape(groups * ways, -1)
    packed = jnp.concatenate(
        [by_destination(summed), by_destination(peak), by_destination(totals)], axis=1
    )
    parts = lax.all_to_all(packed, ("grp", "w"), 0, 0, tiled=True)
    sum_size = group_heads * HD
    parts = parts.reshape(groups, KV, -1)
    part_sums = parts[:, :, :sum_size].reshape(groups, KV, group_heads, HD)
    part_peaks = parts[:, :, sum_size : sum_size + group_heads]
    part_totals = parts[:, :, sum_size + group_heads :]
    joined = jnp.max(part_peaks, axis=0)
    scales = jnp.exp(part_peaks - joined[None])
    merged_totals = jnp.sum(part_totals * scales, axis=0)
    merged_sums = jnp.sum(part_sums * scales[..., None], axis=0)
    attended = (merged_sums / merged_totals[..., None]).reshape(1, H * HD)
    attended = jnp.broadcast_to(attended[None], (groups,) + attended.shape)
    attended = lax.all_to_all(attended, "grp", 0, 0, tiled=True)
    return attended.reshape(rows, H * HD)


def solution(mesh):
    groups, blocks = mesh.shape["grp"], mesh.shape["blk"]
    inner = Mesh(mesh.devices.reshape(groups, blocks // KV, KV), ("grp", "zq", "w"))
    rows = ("zq", "w")
    return jax.shard_map(
        local,
        mesh=inner,
        in_specs=(
            P(rows, None),
            P(("grp",) + rows, None),
            P(("grp",) + rows, None),
            P(("grp",) + rows, None),
            P(("grp",) + rows, None),
            P(),
        ),
        out_specs=P(rows, None),
        check_vma=False,
    )
```

```python
import functools
import math

import jax
import jax.numpy as jnp
from jax import lax
from jax.experimental import pallas as pl
from jax.experimental.pallas import tpu as pltpu
from jax.sharding import Mesh
from jax.sharding import PartitionSpec as P

H = 64
KV = 8
HD = 128


def split_product(weights, values):
    rounded = lax.reduce_precision(weights, exponent_bits=8, mantissa_bits=7)
    high = rounded.astype(jnp.bfloat16)
    low = (weights - rounded).astype(jnp.bfloat16)
    spec = "rgp,pd->rgd"
    return jnp.einsum(spec, high, values, preferred_element_type=jnp.float32) + jnp.einsum(
        spec, low, values, preferred_element_type=jnp.float32
    )


def attend_kernel(inverse_root, query_ref, key_ref, value_ref, sum_ref, peak_ref, total_ref):
    scores = lax.dot_general(
        query_ref[...],
        key_ref[...],
        (((1,), (1,)), ((), ())),
        preferred_element_type=jnp.float32,
    ) * inverse_root
    peak = jnp.max(scores, axis=1, keepdims=True)
    weights = jnp.exp(scores - peak)
    total_ref[...] = jnp.sum(weights, axis=1, keepdims=True)
    peak_ref[...] = peak
    high = weights.astype(jnp.bfloat16)
    low = (weights - high.astype(jnp.float32)).astype(jnp.bfloat16)
    values = value_ref[...]
    sum_ref[...] = jnp.dot(high, values, preferred_element_type=jnp.float32) + jnp.dot(
        low, values, preferred_element_type=jnp.float32
    )


def attend_prefix(query_rows, keys, values, inverse_root):
    count, width = query_rows.shape
    length = keys.shape[0]
    tile = 256
    return pl.pallas_call(
        functools.partial(attend_kernel, inverse_root),
        grid=(count // tile,),
        in_specs=[
            pl.BlockSpec((tile, width), lambda i: (i, 0)),
            pl.BlockSpec((length, width), lambda i: (0, 0)),
            pl.BlockSpec((length, width), lambda i: (0, 0)),
        ],
        out_specs=[
            pl.BlockSpec((tile, width), lambda i: (i, 0)),
            pl.BlockSpec((tile, 1), lambda i: (i, 0)),
            pl.BlockSpec((tile, 1), lambda i: (i, 0)),
        ],
        out_shape=[
            jax.ShapeDtypeStruct((count, width), jnp.float32),
            jax.ShapeDtypeStruct((count, 1), jnp.float32),
            jax.ShapeDtypeStruct((count, 1), jnp.float32),
        ],
        compiler_params=pltpu.CompilerParams(vmem_limit_bytes=48 * 1024 * 1024),
        cost_estimate=pl.CostEstimate(
            flops=6 * count * length * width,
            transcendentals=count * length,
            bytes_accessed=2 * count * width + 4 * length * width + 4 * count * (width + 2),
        ),
    )(query_rows, keys, values)


def local(queries, prefix_keys, prefix_values, draft_keys, draft_values, draft_offset):
    group_heads = H // KV
    rows = queries.shape[0]
    positions = prefix_keys.shape[0]
    ways = lax.axis_size("w")
    quarters = lax.axis_size("zq")
    quarter = lax.axis_index("zq")
    group = lax.axis_index("grp")
    inverse_root = 1.0 / math.sqrt(HD)

    query_heads = queries.reshape(rows, KV, group_heads * HD).transpose(1, 0, 2).reshape(KV, -1)
    key_heads = prefix_keys.reshape(positions, KV, HD).transpose(1, 0, 2).reshape(KV, -1)
    value_heads = prefix_values.reshape(positions, KV, HD).transpose(1, 0, 2).reshape(KV, -1)
    draft_key_heads = draft_keys.reshape(KV, HD)
    draft_value_heads = draft_values.reshape(KV, HD)
    send = jnp.concatenate(
        [query_heads, key_heads, draft_key_heads, value_heads, draft_value_heads], axis=1
    )
    got = lax.all_to_all(send, "w", 0, 0, tiled=True)

    query_size = rows * group_heads * HD
    key_size = positions * HD
    cut = [query_size, key_size, HD, key_size, HD]
    starts = [sum(cut[:n]) for n in range(len(cut))]
    query_block = got[:, : query_size].reshape(ways * rows, group_heads, HD)
    keys_here = jnp.concatenate(
        [
            got[:, starts[1] : starts[1] + key_size].reshape(ways * positions, HD),
            got[:, starts[2] : starts[2] + HD],
        ],
        axis=0,
    )
    values_here = jnp.concatenate(
        [
            got[:, starts[3] : starts[3] + key_size].reshape(ways * positions, HD),
            got[:, starts[4] : starts[4] + HD],
        ],
        axis=0,
    )
    local_keys = ways * positions
    both_here = jnp.stack([keys_here, values_here])
    blocks = [both_here] + [
        lax.ppermute(both_here, "zq", [(i, (i + shift) % quarters) for i in range(quarters)])
        for shift in range(1, quarters)
    ]
    both_all = jnp.stack(blocks)
    keys_all, values_all = both_all[:, 0], both_all[:, 1]
    prefix_k = keys_all[:, :local_keys].reshape(-1, HD)
    draft_k = keys_all[:, local_keys:].reshape(-1, HD)
    prefix_v = values_all[:, :local_keys].reshape(-1, HD)
    draft_v = values_all[:, local_keys:].reshape(-1, HD)
    source_quarter = (quarter - lax.iota(jnp.int32, quarters)) % quarters

    block_rows = ways * rows
    query_rows = query_block.reshape(block_rows * group_heads, HD)
    prefix_sum, prefix_peak, prefix_total = attend_prefix(query_rows, prefix_k, prefix_v, inverse_root)
    prefix_sum = prefix_sum.reshape(block_rows, group_heads, HD)
    prefix_peak = prefix_peak.reshape(block_rows, group_heads)
    prefix_total = prefix_total.reshape(block_rows, group_heads)
    scores_draft = jnp.einsum(
        "rgd,jd->rgj", query_block, draft_k, preferred_element_type=jnp.float32
    ) * inverse_root

    block_index = lax.iota(jnp.int32, block_rows)
    query_index = ((block_index // rows) * quarters + quarter) * rows + block_index % rows
    drafts_per_group = quarters * ways
    draft_source = (lax.iota(jnp.int32, ways)[None, :] * quarters + source_quarter[:, None]).reshape(-1)
    key_index = group * drafts_per_group + draft_source
    offsets = lax.dynamic_slice_in_dim(
        draft_offset.reshape(ways, quarters, rows), quarter, 1, axis=1
    ).reshape(block_rows)
    visible = (key_index[None, :] <= query_index[:, None]) & (
        key_index[None, :] >= (query_index - offsets)[:, None]
    )
    visible = visible[:, None, :]
    masked_draft = jnp.where(visible, scores_draft, -jnp.inf)
    peak = jnp.maximum(prefix_peak, jnp.max(masked_draft, axis=2))
    prefix_scale = jnp.exp(prefix_peak - peak)
    weights_draft = jnp.where(visible, jnp.exp(masked_draft - peak[..., None]), 0.0)
    totals = prefix_total * prefix_scale + jnp.sum(weights_draft, axis=2)
    summed = prefix_sum * prefix_scale[..., None] + split_product(weights_draft, draft_v)

    groups = lax.axis_size("grp")
    def by_destination(part):
        part = part.reshape((ways, groups) + part.shape[1:])
        return part.transpose((1, 0) + tuple(range(2, part.ndim))).reshape(groups * ways, -1)
    packed = jnp.concatenate(
        [by_destination(summed), by_destination(peak), by_destination(totals)], axis=1
    )
    parts = lax.all_to_all(packed, ("grp", "w"), 0, 0, tiled=True)
    sum_size = group_heads * HD
    parts = parts.reshape(groups, KV, -1)
    part_sums = parts[:, :, :sum_size].reshape(groups, KV, group_heads, HD)
    part_peaks = parts[:, :, sum_size : sum_size + group_heads]
    part_totals = parts[:, :, sum_size + group_heads :]
    joined = jnp.max(part_peaks, axis=0)
    scales = jnp.exp(part_peaks - joined[None])
    merged_totals = jnp.sum(part_totals * scales, axis=0)
    merged_sums = jnp.sum(part_sums * scales[..., None], axis=0)
    attended = (merged_sums / merged_totals[..., None]).reshape(1, H * HD)
    attended = jnp.broadcast_to(attended[None], (groups,) + attended.shape)
    attended = lax.all_to_all(attended, "grp", 0, 0, tiled=True)
    return attended.reshape(rows, H * HD)


def solution(mesh):
    groups, blocks = mesh.shape["grp"], mesh.shape["blk"]
    inner = Mesh(mesh.devices.reshape(groups, KV, blocks // KV), ("grp", "w", "zq"))
    rows = ("w", "zq")
    return jax.shard_map(
        local,
        mesh=inner,
        in_specs=(
            P(rows, None),
            P(("grp",) + rows, None),
            P(("grp",) + rows, None),
            P(("grp",) + rows, None),
            P(("grp",) + rows, None),
            P(),
        ),
        out_specs=P(rows, None),
        check_vma=False,
    )
```

```python
import functools
import math

import jax
import jax.numpy as jnp
from jax import lax
from jax.experimental import pallas as pl
from jax.experimental.pallas import tpu as pltpu
from jax.sharding import Mesh
from jax.sharding import PartitionSpec as P

H = 64
KV = 8
HD = 128


def split_product(weights, values):
    rounded = lax.reduce_precision(weights, exponent_bits=8, mantissa_bits=7)
    high = rounded.astype(jnp.bfloat16)
    low = (weights - rounded).astype(jnp.bfloat16)
    spec = "rgp,pd->rgd"
    return jnp.einsum(spec, high, values, preferred_element_type=jnp.float32) + jnp.einsum(
        spec, low, values, preferred_element_type=jnp.float32
    )


def attend_kernel(inverse_root, query_ref, key_ref, value_ref, sum_ref, peak_ref, total_ref):
    scores = lax.dot_general(
        query_ref[...],
        key_ref[...],
        (((1,), (1,)), ((), ())),
        preferred_element_type=jnp.float32,
    ) * inverse_root
    peak = jnp.max(scores, axis=1, keepdims=True)
    weights = jnp.exp(scores - peak)
    total_ref[...] = jnp.sum(weights, axis=1, keepdims=True)
    peak_ref[...] = peak
    high = weights.astype(jnp.bfloat16)
    low = (weights - high.astype(jnp.float32)).astype(jnp.bfloat16)
    values = value_ref[...]
    sum_ref[...] = jnp.dot(high, values, preferred_element_type=jnp.float32) + jnp.dot(
        low, values, preferred_element_type=jnp.float32
    )


def attend_prefix(query_rows, keys, values, inverse_root):
    count, width = query_rows.shape
    length = keys.shape[0]
    tile = 256
    return pl.pallas_call(
        functools.partial(attend_kernel, inverse_root),
        grid=(count // tile,),
        in_specs=[
            pl.BlockSpec((tile, width), lambda i: (i, 0)),
            pl.BlockSpec((length, width), lambda i: (0, 0)),
            pl.BlockSpec((length, width), lambda i: (0, 0)),
        ],
        out_specs=[
            pl.BlockSpec((tile, width), lambda i: (i, 0)),
            pl.BlockSpec((tile, 1), lambda i: (i, 0)),
            pl.BlockSpec((tile, 1), lambda i: (i, 0)),
        ],
        out_shape=[
            jax.ShapeDtypeStruct((count, width), jnp.float32),
            jax.ShapeDtypeStruct((count, 1), jnp.float32),
            jax.ShapeDtypeStruct((count, 1), jnp.float32),
        ],
        compiler_params=pltpu.CompilerParams(vmem_limit_bytes=48 * 1024 * 1024),
        cost_estimate=pl.CostEstimate(
            flops=6 * count * length * width,
            transcendentals=count * length,
            bytes_accessed=2 * count * width + 4 * length * width + 4 * count * (width + 2),
        ),
    )(query_rows, keys, values)


def local(queries, prefix_keys, prefix_values, draft_keys, draft_values, draft_offset):
    group_heads = H // KV
    rows = queries.shape[0]
    positions = prefix_keys.shape[0]
    ways = lax.axis_size("w")
    quarters = lax.axis_size("zq")
    quarter = lax.axis_index("zq")
    group = lax.axis_index("grp")
    inverse_root = 1.0 / math.sqrt(HD)

    query_heads = queries.reshape(rows, KV, group_heads * HD).transpose(1, 0, 2).reshape(KV, -1)
    key_heads = prefix_keys.reshape(positions, KV, HD).transpose(1, 0, 2).reshape(KV, -1)
    value_heads = prefix_values.reshape(positions, KV, HD).transpose(1, 0, 2).reshape(KV, -1)
    draft_key_heads = draft_keys.reshape(KV, HD)
    draft_value_heads = draft_values.reshape(KV, HD)
    send = jnp.concatenate(
        [query_heads, key_heads, draft_key_heads, value_heads, draft_value_heads], axis=1
    )
    got = lax.all_to_all(send, "w", 0, 0, tiled=True)

    query_size = rows * group_heads * HD
    key_size = positions * HD
    cut = [query_size, key_size, HD, key_size, HD]
    starts = [sum(cut[:n]) for n in range(len(cut))]
    query_block = got[:, : query_size].reshape(ways * rows, group_heads, HD)
    keys_here = jnp.concatenate(
        [
            got[:, starts[1] : starts[1] + key_size].reshape(ways * positions, HD),
            got[:, starts[2] : starts[2] + HD],
        ],
        axis=0,
    )
    values_here = jnp.concatenate(
        [
            got[:, starts[3] : starts[3] + key_size].reshape(ways * positions, HD),
            got[:, starts[4] : starts[4] + HD],
        ],
        axis=0,
    )
    local_keys = ways * positions
    both_here = jnp.stack([keys_here, values_here])
    blocks = [both_here] + [
        lax.ppermute(both_here, "zq", [(i, (i + shift) % quarters) for i in range(quarters)])
        for shift in range(1, quarters)
    ]
    draft_k = jnp.concatenate([block[0, local_keys:] for block in blocks], axis=0)
    draft_v = jnp.concatenate([block[1, local_keys:] for block in blocks], axis=0)
    source_quarter = (quarter - lax.iota(jnp.int32, quarters)) % quarters

    block_rows = ways * rows
    query_rows = query_block.reshape(block_rows * group_heads, HD)
    pieces = [
        attend_prefix(query_rows, block[0, :local_keys], block[1, :local_keys], inverse_root)
        for block in blocks
    ]
    prefix_peak = functools.reduce(jnp.maximum, [piece[1] for piece in pieces])
    piece_scales = [jnp.exp(piece[1] - prefix_peak) for piece in pieces]
    prefix_total = sum(piece[2] * scale for piece, scale in zip(pieces, piece_scales))
    prefix_sum = sum(piece[0] * scale for piece, scale in zip(pieces, piece_scales))
    prefix_sum = prefix_sum.reshape(block_rows, group_heads, HD)
    prefix_peak = prefix_peak.reshape(block_rows, group_heads)
    prefix_total = prefix_total.reshape(block_rows, group_heads)
    scores_draft = jnp.einsum(
        "rgd,jd->rgj", query_block, draft_k, preferred_element_type=jnp.float32
    ) * inverse_root

    block_index = lax.iota(jnp.int32, block_rows)
    query_index = ((block_index // rows) * quarters + quarter) * rows + block_index % rows
    drafts_per_group = quarters * ways
    draft_source = (lax.iota(jnp.int32, ways)[None, :] * quarters + source_quarter[:, None]).reshape(-1)
    key_index = group * drafts_per_group + draft_source
    offsets = lax.dynamic_slice_in_dim(
        draft_offset.reshape(ways, quarters, rows), quarter, 1, axis=1
    ).reshape(block_rows)
    visible = (key_index[None, :] <= query_index[:, None]) & (
        key_index[None, :] >= (query_index - offsets)[:, None]
    )
    visible = visible[:, None, :]
    masked_draft = jnp.where(visible, scores_draft, -jnp.inf)
    peak = jnp.maximum(prefix_peak, jnp.max(masked_draft, axis=2))
    prefix_scale = jnp.exp(prefix_peak - peak)
    weights_draft = jnp.where(visible, jnp.exp(masked_draft - peak[..., None]), 0.0)
    totals = prefix_total * prefix_scale + jnp.sum(weights_draft, axis=2)
    summed = prefix_sum * prefix_scale[..., None] + split_product(weights_draft, draft_v)

    groups = lax.axis_size("grp")
    def by_destination(part):
        part = part.reshape((ways, groups) + part.shape[1:])
        return part.transpose((1, 0) + tuple(range(2, part.ndim))).reshape(groups * ways, -1)
    packed = jnp.concatenate(
        [by_destination(summed), by_destination(peak), by_destination(totals)], axis=1
    )
    parts = lax.all_to_all(packed, ("grp", "w"), 0, 0, tiled=True)
    sum_size = group_heads * HD
    parts = parts.reshape(groups, KV, -1)
    part_sums = parts[:, :, :sum_size].reshape(groups, KV, group_heads, HD)
    part_peaks = parts[:, :, sum_size : sum_size + group_heads]
    part_totals = parts[:, :, sum_size + group_heads :]
    joined = jnp.max(part_peaks, axis=0)
    scales = jnp.exp(part_peaks - joined[None])
    merged_totals = jnp.sum(part_totals * scales, axis=0)
    merged_sums = jnp.sum(part_sums * scales[..., None], axis=0)
    attended = (merged_sums / merged_totals[..., None]).reshape(1, H * HD)
    attended = jnp.broadcast_to(attended[None], (groups,) + attended.shape)
    attended = lax.all_to_all(attended, "grp", 0, 0, tiled=True)
    return attended.reshape(rows, H * HD)


def solution(mesh):
    groups, blocks = mesh.shape["grp"], mesh.shape["blk"]
    inner = Mesh(mesh.devices.reshape(groups, KV, blocks // KV), ("grp", "w", "zq"))
    rows = ("w", "zq")
    return jax.shard_map(
        local,
        mesh=inner,
        in_specs=(
            P(rows, None),
            P(("grp",) + rows, None),
            P(("grp",) + rows, None),
            P(("grp",) + rows, None),
            P(("grp",) + rows, None),
            P(),
        ),
        out_specs=P(rows, None),
        check_vma=False,
    )
```

```python
import functools
import math

import jax
import jax.numpy as jnp
from jax import lax
from jax.experimental import pallas as pl
from jax.experimental.pallas import tpu as pltpu
from jax.sharding import Mesh
from jax.sharding import PartitionSpec as P

H = 64
KV = 8
HD = 128


def split_product(weights, values):
    rounded = lax.reduce_precision(weights, exponent_bits=8, mantissa_bits=7)
    high = rounded.astype(jnp.bfloat16)
    low = (weights - rounded).astype(jnp.bfloat16)
    spec = "rgp,pd->rgd"
    return jnp.einsum(spec, high, values, preferred_element_type=jnp.float32) + jnp.einsum(
        spec, low, values, preferred_element_type=jnp.float32
    )


def attend_kernel(inverse_root, query_ref, key_ref, value_ref, sum_ref, peak_ref, total_ref):
    scores = lax.dot_general(
        query_ref[...],
        key_ref[...],
        (((1,), (1,)), ((), ())),
        preferred_element_type=jnp.float32,
    ) * inverse_root
    peak = jnp.max(scores, axis=1, keepdims=True)
    weights = jnp.exp(scores - peak)
    total_ref[...] = jnp.sum(weights, axis=1, keepdims=True)
    peak_ref[...] = peak
    high = weights.astype(jnp.bfloat16)
    low = (weights - high.astype(jnp.float32)).astype(jnp.bfloat16)
    values = value_ref[...]
    sum_ref[...] = jnp.dot(high, values, preferred_element_type=jnp.float32) + jnp.dot(
        low, values, preferred_element_type=jnp.float32
    )


def attend_prefix(query_rows, keys, values, inverse_root):
    count, width = query_rows.shape
    length = keys.shape[0]
    tile = 256
    return pl.pallas_call(
        functools.partial(attend_kernel, inverse_root),
        grid=(count // tile,),
        in_specs=[
            pl.BlockSpec((tile, width), lambda i: (i, 0)),
            pl.BlockSpec((length, width), lambda i: (0, 0)),
            pl.BlockSpec((length, width), lambda i: (0, 0)),
        ],
        out_specs=[
            pl.BlockSpec((tile, width), lambda i: (i, 0)),
            pl.BlockSpec((tile, 1), lambda i: (i, 0)),
            pl.BlockSpec((tile, 1), lambda i: (i, 0)),
        ],
        out_shape=[
            jax.ShapeDtypeStruct((count, width), jnp.float32),
            jax.ShapeDtypeStruct((count, 1), jnp.float32),
            jax.ShapeDtypeStruct((count, 1), jnp.float32),
        ],
        compiler_params=pltpu.CompilerParams(vmem_limit_bytes=48 * 1024 * 1024),
        cost_estimate=pl.CostEstimate(
            flops=6 * count * length * width,
            transcendentals=count * length,
            bytes_accessed=2 * count * width + 4 * length * width + 4 * count * (width + 2),
        ),
    )(query_rows, keys, values)


def local(queries, prefix_keys, prefix_values, draft_keys, draft_values, draft_offset):
    group_heads = H // KV
    rows = queries.shape[0]
    positions = prefix_keys.shape[0]
    ways = lax.axis_size("w")
    quarters = lax.axis_size("zq")
    quarter = lax.axis_index("zq")
    group = lax.axis_index("grp")
    inverse_root = 1.0 / math.sqrt(HD)

    query_heads = queries.reshape(rows, KV, group_heads * HD).transpose(1, 0, 2).reshape(KV, -1)
    key_heads = prefix_keys.reshape(positions, KV, HD).transpose(1, 0, 2).reshape(KV, -1)
    value_heads = prefix_values.reshape(positions, KV, HD).transpose(1, 0, 2).reshape(KV, -1)
    draft_key_heads = draft_keys.reshape(KV, HD)
    draft_value_heads = draft_values.reshape(KV, HD)
    send = jnp.concatenate([key_heads, draft_key_heads, value_heads, draft_value_heads], axis=1)
    got = lax.all_to_all(send, "w", 0, 0, tiled=True)

    key_size = positions * HD
    cut = [key_size, HD, key_size, HD]
    starts = [sum(cut[:n]) for n in range(len(cut))]
    keys_here = jnp.concatenate(
        [
            got[:, starts[0] : starts[0] + key_size].reshape(ways * positions, HD),
            got[:, starts[1] : starts[1] + HD],
        ],
        axis=0,
    )
    values_here = jnp.concatenate(
        [
            got[:, starts[2] : starts[2] + key_size].reshape(ways * positions, HD),
            got[:, starts[3] : starts[3] + HD],
        ],
        axis=0,
    )
    both_here = jnp.stack([keys_here, values_here])
    query_heads, both_here = lax.optimization_barrier((query_heads, both_here))
    query_block = lax.all_to_all(query_heads, "w", 0, 0, tiled=True)
    query_block = query_block.reshape(ways * rows, group_heads, HD)
    local_keys = ways * positions
    blocks = [both_here] + [
        lax.ppermute(both_here, "zq", [(i, (i + shift) % quarters) for i in range(quarters)])
        for shift in range(1, quarters)
    ]
    draft_k = jnp.concatenate([block[0, local_keys:] for block in blocks], axis=0)
    draft_v = jnp.concatenate([block[1, local_keys:] for block in blocks], axis=0)
    source_quarter = (quarter - lax.iota(jnp.int32, quarters)) % quarters

    block_rows = ways * rows
    query_rows = query_block.reshape(block_rows * group_heads, HD)
    pieces = [
        attend_prefix(query_rows, block[0, :local_keys], block[1, :local_keys], inverse_root)
        for block in blocks
    ]
    prefix_peak = functools.reduce(jnp.maximum, [piece[1] for piece in pieces])
    piece_scales = [jnp.exp(piece[1] - prefix_peak) for piece in pieces]
    prefix_total = sum(piece[2] * scale for piece, scale in zip(pieces, piece_scales))
    prefix_sum = sum(piece[0] * scale for piece, scale in zip(pieces, piece_scales))
    prefix_sum = prefix_sum.reshape(block_rows, group_heads, HD)
    prefix_peak = prefix_peak.reshape(block_rows, group_heads)
    prefix_total = prefix_total.reshape(block_rows, group_heads)
    scores_draft = jnp.einsum(
        "rgd,jd->rgj", query_block, draft_k, preferred_element_type=jnp.float32
    ) * inverse_root

    block_index = lax.iota(jnp.int32, block_rows)
    query_index = ((block_index // rows) * quarters + quarter) * rows + block_index % rows
    drafts_per_group = quarters * ways
    draft_source = (lax.iota(jnp.int32, ways)[None, :] * quarters + source_quarter[:, None]).reshape(-1)
    key_index = group * drafts_per_group + draft_source
    offsets = lax.dynamic_slice_in_dim(
        draft_offset.reshape(ways, quarters, rows), quarter, 1, axis=1
    ).reshape(block_rows)
    visible = (key_index[None, :] <= query_index[:, None]) & (
        key_index[None, :] >= (query_index - offsets)[:, None]
    )
    visible = visible[:, None, :]
    masked_draft = jnp.where(visible, scores_draft, -jnp.inf)
    peak = jnp.maximum(prefix_peak, jnp.max(masked_draft, axis=2))
    prefix_scale = jnp.exp(prefix_peak - peak)
    weights_draft = jnp.where(visible, jnp.exp(masked_draft - peak[..., None]), 0.0)
    totals = prefix_total * prefix_scale + jnp.sum(weights_draft, axis=2)
    summed = prefix_sum * prefix_scale[..., None] + split_product(weights_draft, draft_v)

    groups = lax.axis_size("grp")
    def by_destination(part):
        part = part.reshape((ways, groups) + part.shape[1:])
        return part.transpose((1, 0) + tuple(range(2, part.ndim))).reshape(groups * ways, -1)
    packed = jnp.concatenate(
        [by_destination(summed), by_destination(peak), by_destination(totals)], axis=1
    )
    parts = lax.all_to_all(packed, ("grp", "w"), 0, 0, tiled=True)
    sum_size = group_heads * HD
    parts = parts.reshape(groups, KV, -1)
    part_sums = parts[:, :, :sum_size].reshape(groups, KV, group_heads, HD)
    part_peaks = parts[:, :, sum_size : sum_size + group_heads]
    part_totals = parts[:, :, sum_size + group_heads :]
    joined = jnp.max(part_peaks, axis=0)
    scales = jnp.exp(part_peaks - joined[None])
    merged_totals = jnp.sum(part_totals * scales, axis=0)
    merged_sums = jnp.sum(part_sums * scales[..., None], axis=0)
    attended = (merged_sums / merged_totals[..., None]).reshape(1, H * HD)
    attended = jnp.broadcast_to(attended[None], (groups,) + attended.shape)
    attended = lax.all_to_all(attended, "grp", 0, 0, tiled=True)
    return attended.reshape(rows, H * HD)


def solution(mesh):
    groups, blocks = mesh.shape["grp"], mesh.shape["blk"]
    inner = Mesh(mesh.devices.reshape(groups, KV, blocks // KV), ("grp", "w", "zq"))
    rows = ("w", "zq")
    return jax.shard_map(
        local,
        mesh=inner,
        in_specs=(
            P(rows, None),
            P(("grp",) + rows, None),
            P(("grp",) + rows, None),
            P(("grp",) + rows, None),
            P(("grp",) + rows, None),
            P(),
        ),
        out_specs=P(rows, None),
        check_vma=False,
    )
```

```python
import functools
import math

import jax
import jax.numpy as jnp
from jax import lax
from jax.experimental import pallas as pl
from jax.experimental.pallas import tpu as pltpu
from jax.sharding import Mesh
from jax.sharding import PartitionSpec as P

H = 64
KV = 8
HD = 128


def split_product(weights, values):
    rounded = lax.reduce_precision(weights, exponent_bits=8, mantissa_bits=7)
    high = rounded.astype(jnp.bfloat16)
    low = (weights - rounded).astype(jnp.bfloat16)
    spec = "rgp,pd->rgd"
    return jnp.einsum(spec, high, values, preferred_element_type=jnp.float32) + jnp.einsum(
        spec, low, values, preferred_element_type=jnp.float32
    )


def attend_kernel(
    inverse_root, query_ref, key_ref, value_ref, sum_in, peak_in, total_in, sum_ref, peak_ref, total_ref
):
    scores = lax.dot_general(
        query_ref[...],
        key_ref[...],
        (((1,), (1,)), ((), ())),
        preferred_element_type=jnp.float32,
    ) * inverse_root
    old_peak = peak_in[...]
    peak = jnp.maximum(old_peak, jnp.max(scores, axis=1, keepdims=True))
    scale = jnp.exp(old_peak - peak)
    weights = jnp.exp(scores - peak)
    total_ref[...] = total_in[...] * scale + jnp.sum(weights, axis=1, keepdims=True)
    peak_ref[...] = peak
    high = weights.astype(jnp.bfloat16)
    low = (weights - high.astype(jnp.float32)).astype(jnp.bfloat16)
    values = value_ref[...]
    sum_ref[...] = sum_in[...] * scale + (
        jnp.dot(high, values, preferred_element_type=jnp.float32)
        + jnp.dot(low, values, preferred_element_type=jnp.float32)
    )


def attend_prefix(query_rows, keys, values, inverse_root, state):
    count, width = query_rows.shape
    length = keys.shape[0]
    tile = 256
    row_block = pl.BlockSpec((tile, width), lambda i: (i, 0))
    column_block = pl.BlockSpec((tile, 1), lambda i: (i, 0))
    whole = pl.BlockSpec((length, width), lambda i: (0, 0))
    return pl.pallas_call(
        functools.partial(attend_kernel, inverse_root),
        grid=(count // tile,),
        in_specs=[row_block, whole, whole, row_block, column_block, column_block],
        out_specs=[row_block, column_block, column_block],
        out_shape=[
            jax.ShapeDtypeStruct((count, width), jnp.float32),
            jax.ShapeDtypeStruct((count, 1), jnp.float32),
            jax.ShapeDtypeStruct((count, 1), jnp.float32),
        ],
        input_output_aliases={3: 0, 4: 1, 5: 2},
        compiler_params=pltpu.CompilerParams(vmem_limit_bytes=48 * 1024 * 1024),
        cost_estimate=pl.CostEstimate(
            flops=6 * count * length * width,
            transcendentals=count * length,
            bytes_accessed=2 * count * width + 4 * length * width + 8 * count * (width + 2),
        ),
    )(query_rows, keys, values, *state)


def local(queries, prefix_keys, prefix_values, draft_keys, draft_values, draft_offset):
    group_heads = H // KV
    rows = queries.shape[0]
    positions = prefix_keys.shape[0]
    ways = lax.axis_size("w")
    quarters = lax.axis_size("zq")
    quarter = lax.axis_index("zq")
    group = lax.axis_index("grp")
    inverse_root = 1.0 / math.sqrt(HD)

    query_heads = queries.reshape(rows, KV, group_heads * HD).transpose(1, 0, 2).reshape(KV, -1)
    key_heads = prefix_keys.reshape(positions, KV, HD).transpose(1, 0, 2).reshape(KV, -1)
    value_heads = prefix_values.reshape(positions, KV, HD).transpose(1, 0, 2).reshape(KV, -1)
    draft_key_heads = draft_keys.reshape(KV, HD)
    draft_value_heads = draft_values.reshape(KV, HD)
    send = jnp.concatenate(
        [query_heads, key_heads, draft_key_heads, value_heads, draft_value_heads], axis=1
    )
    got = lax.all_to_all(send, "w", 0, 0, tiled=True)

    query_size = rows * group_heads * HD
    key_size = positions * HD
    cut = [query_size, key_size, HD, key_size, HD]
    starts = [sum(cut[:n]) for n in range(len(cut))]
    query_block = got[:, : query_size].reshape(ways * rows, group_heads, HD)
    keys_here = jnp.concatenate(
        [
            got[:, starts[1] : starts[1] + key_size].reshape(ways * positions, HD),
            got[:, starts[2] : starts[2] + HD],
        ],
        axis=0,
    )
    values_here = jnp.concatenate(
        [
            got[:, starts[3] : starts[3] + key_size].reshape(ways * positions, HD),
            got[:, starts[4] : starts[4] + HD],
        ],
        axis=0,
    )
    local_keys = ways * positions
    both_here = jnp.stack([keys_here, values_here])
    blocks = [both_here] + [
        lax.ppermute(both_here, "zq", [(i, (i + shift) % quarters) for i in range(quarters)])
        for shift in range(1, quarters)
    ]
    draft_k = jnp.concatenate([block[0, local_keys:] for block in blocks], axis=0)
    draft_v = jnp.concatenate([block[1, local_keys:] for block in blocks], axis=0)
    source_quarter = (quarter - lax.iota(jnp.int32, quarters)) % quarters

    block_rows = ways * rows
    query_rows = query_block.reshape(block_rows * group_heads, HD)
    rows_total = block_rows * group_heads
    state = (
        jnp.zeros((rows_total, HD), jnp.float32),
        jnp.full((rows_total, 1), -jnp.inf, jnp.float32),
        jnp.zeros((rows_total, 1), jnp.float32),
    )
    for block in blocks:
        state = attend_prefix(query_rows, block[0, :local_keys], block[1, :local_keys], inverse_root, state)
    prefix_sum, prefix_peak, prefix_total = state
    prefix_sum = prefix_sum.reshape(block_rows, group_heads, HD)
    prefix_peak = prefix_peak.reshape(block_rows, group_heads)
    prefix_total = prefix_total.reshape(block_rows, group_heads)
    scores_draft = jnp.einsum(
        "rgd,jd->rgj", query_block, draft_k, preferred_element_type=jnp.float32
    ) * inverse_root

    block_index = lax.iota(jnp.int32, block_rows)
    query_index = ((block_index // rows) * quarters + quarter) * rows + block_index % rows
    drafts_per_group = quarters * ways
    draft_source = (lax.iota(jnp.int32, ways)[None, :] * quarters + source_quarter[:, None]).reshape(-1)
    key_index = group * drafts_per_group + draft_source
    offsets = lax.dynamic_slice_in_dim(
        draft_offset.reshape(ways, quarters, rows), quarter, 1, axis=1
    ).reshape(block_rows)
    visible = (key_index[None, :] <= query_index[:, None]) & (
        key_index[None, :] >= (query_index - offsets)[:, None]
    )
    visible = visible[:, None, :]
    masked_draft = jnp.where(visible, scores_draft, -jnp.inf)
    peak = jnp.maximum(prefix_peak, jnp.max(masked_draft, axis=2))
    prefix_scale = jnp.exp(prefix_peak - peak)
    weights_draft = jnp.where(visible, jnp.exp(masked_draft - peak[..., None]), 0.0)
    totals = prefix_total * prefix_scale + jnp.sum(weights_draft, axis=2)
    summed = prefix_sum * prefix_scale[..., None] + split_product(weights_draft, draft_v)

    groups = lax.axis_size("grp")
    def by_destination(part):
        part = part.reshape((ways, groups) + part.shape[1:])
        return part.transpose((1, 0) + tuple(range(2, part.ndim))).reshape(groups * ways, -1)
    packed = jnp.concatenate(
        [by_destination(summed), by_destination(peak), by_destination(totals)], axis=1
    )
    parts = lax.all_to_all(packed, ("grp", "w"), 0, 0, tiled=True)
    sum_size = group_heads * HD
    parts = parts.reshape(groups, KV, -1)
    part_sums = parts[:, :, :sum_size].reshape(groups, KV, group_heads, HD)
    part_peaks = parts[:, :, sum_size : sum_size + group_heads]
    part_totals = parts[:, :, sum_size + group_heads :]
    joined = jnp.max(part_peaks, axis=0)
    scales = jnp.exp(part_peaks - joined[None])
    merged_totals = jnp.sum(part_totals * scales, axis=0)
    merged_sums = jnp.sum(part_sums * scales[..., None], axis=0)
    attended = (merged_sums / merged_totals[..., None]).reshape(1, H * HD)
    attended = jnp.broadcast_to(attended[None], (groups,) + attended.shape)
    attended = lax.all_to_all(attended, "grp", 0, 0, tiled=True)
    return attended.reshape(rows, H * HD)


def solution(mesh):
    groups, blocks = mesh.shape["grp"], mesh.shape["blk"]
    inner = Mesh(mesh.devices.reshape(groups, KV, blocks // KV), ("grp", "w", "zq"))
    rows = ("w", "zq")
    return jax.shard_map(
        local,
        mesh=inner,
        in_specs=(
            P(rows, None),
            P(("grp",) + rows, None),
            P(("grp",) + rows, None),
            P(("grp",) + rows, None),
            P(("grp",) + rows, None),
            P(),
        ),
        out_specs=P(rows, None),
        check_vma=False,
    )
```

```python
import functools
import math

import jax
import jax.numpy as jnp
from jax import lax
from jax.experimental import pallas as pl
from jax.experimental.pallas import tpu as pltpu
from jax.sharding import Mesh
from jax.sharding import PartitionSpec as P

H = 64
KV = 8
HD = 128


def split_product(weights, values):
    rounded = lax.reduce_precision(weights, exponent_bits=8, mantissa_bits=7)
    high = rounded.astype(jnp.bfloat16)
    low = (weights - rounded).astype(jnp.bfloat16)
    spec = "rgp,pd->rgd"
    return jnp.einsum(spec, high, values, preferred_element_type=jnp.float32) + jnp.einsum(
        spec, low, values, preferred_element_type=jnp.float32
    )


def attend_kernel(inverse_root, query_ref, key_ref, value_ref, sum_ref, peak_ref, total_ref):
    scores = lax.dot_general(
        query_ref[...],
        key_ref[...],
        (((1,), (1,)), ((), ())),
        preferred_element_type=jnp.float32,
    ) * inverse_root
    peak = jnp.max(scores, axis=1, keepdims=True)
    weights = jnp.exp(scores - peak)
    total_ref[...] = jnp.sum(weights, axis=1, keepdims=True)
    peak_ref[...] = peak
    high = weights.astype(jnp.bfloat16)
    low = (weights - high.astype(jnp.float32)).astype(jnp.bfloat16)
    values = value_ref[...]
    sum_ref[...] = jnp.dot(high, values, preferred_element_type=jnp.float32) + jnp.dot(
        low, values, preferred_element_type=jnp.float32
    )


def attend_prefix(query_rows, keys, values, inverse_root):
    count, width = query_rows.shape
    length = keys.shape[0]
    tile = 512
    return pl.pallas_call(
        functools.partial(attend_kernel, inverse_root),
        grid=(count // tile,),
        in_specs=[
            pl.BlockSpec((tile, width), lambda i: (i, 0)),
            pl.BlockSpec((length, width), lambda i: (0, 0)),
            pl.BlockSpec((length, width), lambda i: (0, 0)),
        ],
        out_specs=[
            pl.BlockSpec((tile, width), lambda i: (i, 0)),
            pl.BlockSpec((tile, 1), lambda i: (i, 0)),
            pl.BlockSpec((tile, 1), lambda i: (i, 0)),
        ],
        out_shape=[
            jax.ShapeDtypeStruct((count, width), jnp.float32),
            jax.ShapeDtypeStruct((count, 1), jnp.float32),
            jax.ShapeDtypeStruct((count, 1), jnp.float32),
        ],
        compiler_params=pltpu.CompilerParams(vmem_limit_bytes=48 * 1024 * 1024),
        cost_estimate=pl.CostEstimate(
            flops=6 * count * length * width,
            transcendentals=count * length,
            bytes_accessed=2 * count * width + 4 * length * width + 4 * count * (width + 2),
        ),
    )(query_rows, keys, values)


def local(queries, prefix_keys, prefix_values, draft_keys, draft_values, draft_offset):
    group_heads = H // KV
    rows = queries.shape[0]
    positions = prefix_keys.shape[0]
    ways = lax.axis_size("w")
    quarters = lax.axis_size("zq")
    quarter = lax.axis_index("zq")
    group = lax.axis_index("grp")
    inverse_root = 1.0 / math.sqrt(HD)

    query_heads = queries.reshape(rows, KV, group_heads * HD).transpose(1, 0, 2).reshape(KV, -1)
    key_heads = prefix_keys.reshape(positions, KV, HD).transpose(1, 0, 2).reshape(KV, -1)
    value_heads = prefix_values.reshape(positions, KV, HD).transpose(1, 0, 2).reshape(KV, -1)
    draft_key_heads = draft_keys.reshape(KV, HD)
    draft_value_heads = draft_values.reshape(KV, HD)
    send = jnp.concatenate(
        [query_heads, key_heads, draft_key_heads, value_heads, draft_value_heads], axis=1
    )
    got = lax.all_to_all(send, "w", 0, 0, tiled=True)

    query_size = rows * group_heads * HD
    key_size = positions * HD
    cut = [query_size, key_size, HD, key_size, HD]
    starts = [sum(cut[:n]) for n in range(len(cut))]
    query_block = got[:, : query_size].reshape(ways * rows, group_heads, HD)
    keys_here = jnp.concatenate(
        [
            got[:, starts[1] : starts[1] + key_size].reshape(ways * positions, HD),
            got[:, starts[2] : starts[2] + HD],
        ],
        axis=0,
    )
    values_here = jnp.concatenate(
        [
            got[:, starts[3] : starts[3] + key_size].reshape(ways * positions, HD),
            got[:, starts[4] : starts[4] + HD],
        ],
        axis=0,
    )
    local_keys = ways * positions
    both_here = jnp.stack([keys_here, values_here])
    blocks = [both_here] + [
        lax.ppermute(both_here, "zq", [(i, (i + shift) % quarters) for i in range(quarters)])
        for shift in range(1, quarters)
    ]
    draft_k = jnp.concatenate([block[0, local_keys:] for block in blocks], axis=0)
    draft_v = jnp.concatenate([block[1, local_keys:] for block in blocks], axis=0)
    source_quarter = (quarter - lax.iota(jnp.int32, quarters)) % quarters

    block_rows = ways * rows
    query_rows = query_block.reshape(block_rows * group_heads, HD)
    pieces = [
        attend_prefix(query_rows, block[0, :local_keys], block[1, :local_keys], inverse_root)
        for block in blocks
    ]
    prefix_peak = functools.reduce(jnp.maximum, [piece[1] for piece in pieces])
    piece_scales = [jnp.exp(piece[1] - prefix_peak) for piece in pieces]
    prefix_total = sum(piece[2] * scale for piece, scale in zip(pieces, piece_scales))
    prefix_sum = sum(piece[0] * scale for piece, scale in zip(pieces, piece_scales))
    prefix_sum = prefix_sum.reshape(block_rows, group_heads, HD)
    prefix_peak = prefix_peak.reshape(block_rows, group_heads)
    prefix_total = prefix_total.reshape(block_rows, group_heads)
    scores_draft = jnp.einsum(
        "rgd,jd->rgj", query_block, draft_k, preferred_element_type=jnp.float32
    ) * inverse_root

    block_index = lax.iota(jnp.int32, block_rows)
    query_index = ((block_index // rows) * quarters + quarter) * rows + block_index % rows
    drafts_per_group = quarters * ways
    draft_source = (lax.iota(jnp.int32, ways)[None, :] * quarters + source_quarter[:, None]).reshape(-1)
    key_index = group * drafts_per_group + draft_source
    offsets = lax.dynamic_slice_in_dim(
        draft_offset.reshape(ways, quarters, rows), quarter, 1, axis=1
    ).reshape(block_rows)
    visible = (key_index[None, :] <= query_index[:, None]) & (
        key_index[None, :] >= (query_index - offsets)[:, None]
    )
    visible = visible[:, None, :]
    masked_draft = jnp.where(visible, scores_draft, -jnp.inf)
    peak = jnp.maximum(prefix_peak, jnp.max(masked_draft, axis=2))
    prefix_scale = jnp.exp(prefix_peak - peak)
    weights_draft = jnp.where(visible, jnp.exp(masked_draft - peak[..., None]), 0.0)
    totals = prefix_total * prefix_scale + jnp.sum(weights_draft, axis=2)
    summed = prefix_sum * prefix_scale[..., None] + split_product(weights_draft, draft_v)

    groups = lax.axis_size("grp")
    def by_destination(part):
        part = part.reshape((ways, groups) + part.shape[1:])
        return part.transpose((1, 0) + tuple(range(2, part.ndim))).reshape(groups * ways, -1)
    packed = jnp.concatenate(
        [by_destination(summed), by_destination(peak), by_destination(totals)], axis=1
    )
    parts = lax.all_to_all(packed, ("grp", "w"), 0, 0, tiled=True)
    sum_size = group_heads * HD
    parts = parts.reshape(groups, KV, -1)
    part_sums = parts[:, :, :sum_size].reshape(groups, KV, group_heads, HD)
    part_peaks = parts[:, :, sum_size : sum_size + group_heads]
    part_totals = parts[:, :, sum_size + group_heads :]
    joined = jnp.max(part_peaks, axis=0)
    scales = jnp.exp(part_peaks - joined[None])
    merged_totals = jnp.sum(part_totals * scales, axis=0)
    merged_sums = jnp.sum(part_sums * scales[..., None], axis=0)
    attended = (merged_sums / merged_totals[..., None]).reshape(1, H * HD)
    attended = jnp.broadcast_to(attended[None], (groups,) + attended.shape)
    attended = lax.all_to_all(attended, "grp", 0, 0, tiled=True)
    return attended.reshape(rows, H * HD)


def solution(mesh):
    groups, blocks = mesh.shape["grp"], mesh.shape["blk"]
    inner = Mesh(mesh.devices.reshape(groups, KV, blocks // KV), ("grp", "w", "zq"))
    rows = ("w", "zq")
    return jax.shard_map(
        local,
        mesh=inner,
        in_specs=(
            P(rows, None),
            P(("grp",) + rows, None),
            P(("grp",) + rows, None),
            P(("grp",) + rows, None),
            P(("grp",) + rows, None),
            P(),
        ),
        out_specs=P(rows, None),
        check_vma=False,
    )
```

```python
import functools
import math

import jax
import jax.numpy as jnp
from jax import lax
from jax.experimental import pallas as pl
from jax.experimental.pallas import tpu as pltpu
from jax.sharding import Mesh
from jax.sharding import PartitionSpec as P

H = 64
KV = 8
HD = 128


def split_product(weights, values):
    rounded = lax.reduce_precision(weights, exponent_bits=8, mantissa_bits=7)
    high = rounded.astype(jnp.bfloat16)
    low = (weights - rounded).astype(jnp.bfloat16)
    spec = "rgp,pd->rgd"
    return jnp.einsum(spec, high, values, preferred_element_type=jnp.float32) + jnp.einsum(
        spec, low, values, preferred_element_type=jnp.float32
    )


def attend_kernel(inverse_root, query_ref, key_ref, value_ref, sum_ref, peak_ref, total_ref):
    scores = lax.dot_general(
        query_ref[...],
        key_ref[...],
        (((1,), (1,)), ((), ())),
        preferred_element_type=jnp.float32,
    ) * inverse_root
    peak = jnp.max(scores, axis=1, keepdims=True)
    weights = jnp.exp(scores - peak)
    total_ref[...] = jnp.sum(weights, axis=1, keepdims=True)
    peak_ref[...] = peak
    high = weights.astype(jnp.bfloat16)
    low = (weights - high.astype(jnp.float32)).astype(jnp.bfloat16)
    values = value_ref[...]
    sum_ref[...] = jnp.dot(high, values, preferred_element_type=jnp.float32) + jnp.dot(
        low, values, preferred_element_type=jnp.float32
    )


def attend_prefix(query_rows, keys, values, inverse_root):
    count, width = query_rows.shape
    length = keys.shape[0]
    tile = 256
    return pl.pallas_call(
        functools.partial(attend_kernel, inverse_root),
        grid=(count // tile,),
        in_specs=[
            pl.BlockSpec((tile, width), lambda i: (i, 0)),
            pl.BlockSpec((length, width), lambda i: (0, 0)),
            pl.BlockSpec((length, width), lambda i: (0, 0)),
        ],
        out_specs=[
            pl.BlockSpec((tile, width), lambda i: (i, 0)),
            pl.BlockSpec((tile, 1), lambda i: (i, 0)),
            pl.BlockSpec((tile, 1), lambda i: (i, 0)),
        ],
        out_shape=[
            jax.ShapeDtypeStruct((count, width), jnp.float32),
            jax.ShapeDtypeStruct((count, 1), jnp.float32),
            jax.ShapeDtypeStruct((count, 1), jnp.float32),
        ],
        compiler_params=pltpu.CompilerParams(vmem_limit_bytes=48 * 1024 * 1024),
        cost_estimate=pl.CostEstimate(
            flops=6 * count * length * width,
            transcendentals=count * length,
            bytes_accessed=2 * count * width + 4 * length * width + 4 * count * (width + 2),
        ),
    )(query_rows, keys, values)


def local(queries, prefix_keys, prefix_values, draft_keys, draft_values, draft_offset):
    group_heads = H // KV
    rows = queries.shape[0]
    positions = prefix_keys.shape[0]
    ways = lax.axis_size("w")
    quarters = lax.axis_size("zq")
    quarter = lax.axis_index("zq")
    group = lax.axis_index("grp")
    inverse_root = 1.0 / math.sqrt(HD)

    query_heads = queries.reshape(rows, KV, group_heads * HD).transpose(1, 0, 2).reshape(KV, -1)
    key_heads = prefix_keys.reshape(positions, KV, HD).transpose(1, 0, 2).reshape(KV, -1)
    value_heads = prefix_values.reshape(positions, KV, HD).transpose(1, 0, 2).reshape(KV, -1)
    draft_key_heads = draft_keys.reshape(KV, HD)
    draft_value_heads = draft_values.reshape(KV, HD)
    send = jnp.concatenate(
        [query_heads, key_heads, draft_key_heads, value_heads, draft_value_heads], axis=1
    )
    got = lax.all_to_all(send, "w", 0, 0, tiled=True)

    query_size = rows * group_heads * HD
    key_size = positions * HD
    cut = [query_size, key_size, HD, key_size, HD]
    starts = [sum(cut[:n]) for n in range(len(cut))]
    query_block = got[:, : query_size].reshape(ways * rows, group_heads, HD)
    keys_here = jnp.concatenate(
        [
            got[:, starts[1] : starts[1] + key_size].reshape(ways * positions, HD),
            got[:, starts[2] : starts[2] + HD],
        ],
        axis=0,
    )
    values_here = jnp.concatenate(
        [
            got[:, starts[3] : starts[3] + key_size].reshape(ways * positions, HD),
            got[:, starts[4] : starts[4] + HD],
        ],
        axis=0,
    )
    local_keys = ways * positions
    both_here = jnp.stack([keys_here, values_here])
    shifts = [0] + [shift for shift in range(1, quarters) if 2 * shift != quarters]
    shifts += [shift for shift in range(1, quarters) if 2 * shift == quarters]
    blocks = [both_here] + [
        lax.ppermute(both_here, "zq", [(i, (i + shift) % quarters) for i in range(quarters)])
        for shift in shifts[1:]
    ]
    draft_k = jnp.concatenate([block[0, local_keys:] for block in blocks], axis=0)
    draft_v = jnp.concatenate([block[1, local_keys:] for block in blocks], axis=0)
    source_quarter = (quarter - jnp.array(shifts, jnp.int32)) % quarters

    block_rows = ways * rows
    query_rows = query_block.reshape(block_rows * group_heads, HD)
    pieces = [
        attend_prefix(query_rows, block[0, :local_keys], block[1, :local_keys], inverse_root)
        for block in blocks
    ]
    prefix_peak = functools.reduce(jnp.maximum, [piece[1] for piece in pieces])
    piece_scales = [jnp.exp(piece[1] - prefix_peak) for piece in pieces]
    prefix_total = sum(piece[2] * scale for piece, scale in zip(pieces, piece_scales))
    prefix_sum = sum(piece[0] * scale for piece, scale in zip(pieces, piece_scales))
    prefix_sum = prefix_sum.reshape(block_rows, group_heads, HD)
    prefix_peak = prefix_peak.reshape(block_rows, group_heads)
    prefix_total = prefix_total.reshape(block_rows, group_heads)
    scores_draft = jnp.einsum(
        "rgd,jd->rgj", query_block, draft_k, preferred_element_type=jnp.float32
    ) * inverse_root

    block_index = lax.iota(jnp.int32, block_rows)
    query_index = ((block_index // rows) * quarters + quarter) * rows + block_index % rows
    drafts_per_group = quarters * ways
    draft_source = (lax.iota(jnp.int32, ways)[None, :] * quarters + source_quarter[:, None]).reshape(-1)
    key_index = group * drafts_per_group + draft_source
    offsets = lax.dynamic_slice_in_dim(
        draft_offset.reshape(ways, quarters, rows), quarter, 1, axis=1
    ).reshape(block_rows)
    visible = (key_index[None, :] <= query_index[:, None]) & (
        key_index[None, :] >= (query_index - offsets)[:, None]
    )
    visible = visible[:, None, :]
    masked_draft = jnp.where(visible, scores_draft, -jnp.inf)
    peak = jnp.maximum(prefix_peak, jnp.max(masked_draft, axis=2))
    prefix_scale = jnp.exp(prefix_peak - peak)
    weights_draft = jnp.where(visible, jnp.exp(masked_draft - peak[..., None]), 0.0)
    totals = prefix_total * prefix_scale + jnp.sum(weights_draft, axis=2)
    summed = prefix_sum * prefix_scale[..., None] + split_product(weights_draft, draft_v)

    groups = lax.axis_size("grp")
    def by_destination(part):
        part = part.reshape((ways, groups) + part.shape[1:])
        return part.transpose((1, 0) + tuple(range(2, part.ndim))).reshape(groups * ways, -1)
    packed = jnp.concatenate(
        [by_destination(summed), by_destination(peak), by_destination(totals)], axis=1
    )
    parts = lax.all_to_all(packed, ("grp", "w"), 0, 0, tiled=True)
    sum_size = group_heads * HD
    parts = parts.reshape(groups, KV, -1)
    part_sums = parts[:, :, :sum_size].reshape(groups, KV, group_heads, HD)
    part_peaks = parts[:, :, sum_size : sum_size + group_heads]
    part_totals = parts[:, :, sum_size + group_heads :]
    joined = jnp.max(part_peaks, axis=0)
    scales = jnp.exp(part_peaks - joined[None])
    merged_totals = jnp.sum(part_totals * scales, axis=0)
    merged_sums = jnp.sum(part_sums * scales[..., None], axis=0)
    attended = (merged_sums / merged_totals[..., None]).reshape(1, H * HD)
    attended = jnp.broadcast_to(attended[None], (groups,) + attended.shape)
    attended = lax.all_to_all(attended, "grp", 0, 0, tiled=True)
    return attended.reshape(rows, H * HD)


def solution(mesh):
    groups, blocks = mesh.shape["grp"], mesh.shape["blk"]
    inner = Mesh(mesh.devices.reshape(groups, KV, blocks // KV), ("grp", "w", "zq"))
    rows = ("w", "zq")
    return jax.shard_map(
        local,
        mesh=inner,
        in_specs=(
            P(rows, None),
            P(("grp",) + rows, None),
            P(("grp",) + rows, None),
            P(("grp",) + rows, None),
            P(("grp",) + rows, None),
            P(),
        ),
        out_specs=P(rows, None),
        check_vma=False,
    )
```

```python
import functools
import math

import jax
import jax.numpy as jnp
from jax import lax
from jax.experimental import pallas as pl
from jax.experimental.pallas import tpu as pltpu
from jax.sharding import Mesh
from jax.sharding import PartitionSpec as P

H = 64
KV = 8
HD = 128


def split_product(weights, values):
    rounded = lax.reduce_precision(weights, exponent_bits=8, mantissa_bits=7)
    high = rounded.astype(jnp.bfloat16)
    low = (weights - rounded).astype(jnp.bfloat16)
    spec = "rgp,pd->rgd"
    return jnp.einsum(spec, high, values, preferred_element_type=jnp.float32) + jnp.einsum(
        spec, low, values, preferred_element_type=jnp.float32
    )


def attend_kernel(inverse_root, query_ref, key_ref, value_ref, sum_ref, peak_ref, total_ref):
    scores = lax.dot_general(
        query_ref[...],
        key_ref[...],
        (((1,), (1,)), ((), ())),
        preferred_element_type=jnp.float32,
    ) * inverse_root
    peak = jnp.max(scores, axis=1, keepdims=True)
    weights = jnp.exp(scores - peak)
    total_ref[...] = jnp.sum(weights, axis=1, keepdims=True)
    peak_ref[...] = peak
    high = weights.astype(jnp.bfloat16)
    low = (weights - high.astype(jnp.float32)).astype(jnp.bfloat16)
    values = value_ref[...]
    sum_ref[...] = jnp.dot(high, values, preferred_element_type=jnp.float32) + jnp.dot(
        low, values, preferred_element_type=jnp.float32
    )


def attend_prefix(query_rows, keys, values, inverse_root):
    count, width = query_rows.shape
    length = keys.shape[0]
    tile = 128
    return pl.pallas_call(
        functools.partial(attend_kernel, inverse_root),
        grid=(count // tile,),
        in_specs=[
            pl.BlockSpec((tile, width), lambda i: (i, 0)),
            pl.BlockSpec((length, width), lambda i: (0, 0)),
            pl.BlockSpec((length, width), lambda i: (0, 0)),
        ],
        out_specs=[
            pl.BlockSpec((tile, width), lambda i: (i, 0)),
            pl.BlockSpec((tile, 1), lambda i: (i, 0)),
            pl.BlockSpec((tile, 1), lambda i: (i, 0)),
        ],
        out_shape=[
            jax.ShapeDtypeStruct((count, width), jnp.float32),
            jax.ShapeDtypeStruct((count, 1), jnp.float32),
            jax.ShapeDtypeStruct((count, 1), jnp.float32),
        ],
        compiler_params=pltpu.CompilerParams(vmem_limit_bytes=48 * 1024 * 1024),
        cost_estimate=pl.CostEstimate(
            flops=6 * count * length * width,
            transcendentals=count * length,
            bytes_accessed=2 * count * width + 4 * length * width + 4 * count * (width + 2),
        ),
    )(query_rows, keys, values)


def local(queries, prefix_keys, prefix_values, draft_keys, draft_values, draft_offset):
    group_heads = H // KV
    rows = queries.shape[0]
    positions = prefix_keys.shape[0]
    ways = lax.axis_size("w")
    quarters = lax.axis_size("zq")
    quarter = lax.axis_index("zq")
    group = lax.axis_index("grp")
    inverse_root = 1.0 / math.sqrt(HD)

    query_heads = queries.reshape(rows, KV, group_heads * HD).transpose(1, 0, 2).reshape(KV, -1)
    key_heads = prefix_keys.reshape(positions, KV, HD).transpose(1, 0, 2).reshape(KV, -1)
    value_heads = prefix_values.reshape(positions, KV, HD).transpose(1, 0, 2).reshape(KV, -1)
    draft_key_heads = draft_keys.reshape(KV, HD)
    draft_value_heads = draft_values.reshape(KV, HD)
    send = jnp.concatenate(
        [query_heads, key_heads, draft_key_heads, value_heads, draft_value_heads], axis=1
    )
    got = lax.all_to_all(send, "w", 0, 0, tiled=True)

    query_size = rows * group_heads * HD
    key_size = positions * HD
    cut = [query_size, key_size, HD, key_size, HD]
    starts = [sum(cut[:n]) for n in range(len(cut))]
    query_block = got[:, : query_size].reshape(ways * rows, group_heads, HD)
    keys_here = jnp.concatenate(
        [
            got[:, starts[1] : starts[1] + key_size].reshape(ways * positions, HD),
            got[:, starts[2] : starts[2] + HD],
        ],
        axis=0,
    )
    values_here = jnp.concatenate(
        [
            got[:, starts[3] : starts[3] + key_size].reshape(ways * positions, HD),
            got[:, starts[4] : starts[4] + HD],
        ],
        axis=0,
    )
    local_keys = ways * positions
    both_here = jnp.stack([keys_here, values_here])
    blocks = [both_here] + [
        lax.ppermute(both_here, "zq", [(i, (i + shift) % quarters) for i in range(quarters)])
        for shift in range(1, quarters)
    ]
    draft_k = jnp.concatenate([block[0, local_keys:] for block in blocks], axis=0)
    draft_v = jnp.concatenate([block[1, local_keys:] for block in blocks], axis=0)
    source_quarter = (quarter - lax.iota(jnp.int32, quarters)) % quarters

    block_rows = ways * rows
    query_rows = query_block.reshape(block_rows * group_heads, HD)
    pieces = [
        attend_prefix(query_rows, block[0, :local_keys], block[1, :local_keys], inverse_root)
        for block in blocks
    ]
    prefix_peak = functools.reduce(jnp.maximum, [piece[1] for piece in pieces])
    piece_scales = [jnp.exp(piece[1] - prefix_peak) for piece in pieces]
    prefix_total = sum(piece[2] * scale for piece, scale in zip(pieces, piece_scales))
    prefix_sum = sum(piece[0] * scale for piece, scale in zip(pieces, piece_scales))
    prefix_sum = prefix_sum.reshape(block_rows, group_heads, HD)
    prefix_peak = prefix_peak.reshape(block_rows, group_heads)
    prefix_total = prefix_total.reshape(block_rows, group_heads)
    scores_draft = jnp.einsum(
        "rgd,jd->rgj", query_block, draft_k, preferred_element_type=jnp.float32
    ) * inverse_root

    block_index = lax.iota(jnp.int32, block_rows)
    query_index = ((block_index // rows) * quarters + quarter) * rows + block_index % rows
    drafts_per_group = quarters * ways
    draft_source = (lax.iota(jnp.int32, ways)[None, :] * quarters + source_quarter[:, None]).reshape(-1)
    key_index = group * drafts_per_group + draft_source
    offsets = lax.dynamic_slice_in_dim(
        draft_offset.reshape(ways, quarters, rows), quarter, 1, axis=1
    ).reshape(block_rows)
    visible = (key_index[None, :] <= query_index[:, None]) & (
        key_index[None, :] >= (query_index - offsets)[:, None]
    )
    visible = visible[:, None, :]
    masked_draft = jnp.where(visible, scores_draft, -jnp.inf)
    peak = jnp.maximum(prefix_peak, jnp.max(masked_draft, axis=2))
    prefix_scale = jnp.exp(prefix_peak - peak)
    weights_draft = jnp.where(visible, jnp.exp(masked_draft - peak[..., None]), 0.0)
    totals = prefix_total * prefix_scale + jnp.sum(weights_draft, axis=2)
    summed = prefix_sum * prefix_scale[..., None] + split_product(weights_draft, draft_v)

    groups = lax.axis_size("grp")
    def by_destination(part):
        part = part.reshape((ways, groups) + part.shape[1:])
        return part.transpose((1, 0) + tuple(range(2, part.ndim))).reshape(groups * ways, -1)
    packed = jnp.concatenate(
        [by_destination(summed), by_destination(peak), by_destination(totals)], axis=1
    )
    parts = lax.all_to_all(packed, ("grp", "w"), 0, 0, tiled=True)
    sum_size = group_heads * HD
    parts = parts.reshape(groups, KV, -1)
    part_sums = parts[:, :, :sum_size].reshape(groups, KV, group_heads, HD)
    part_peaks = parts[:, :, sum_size : sum_size + group_heads]
    part_totals = parts[:, :, sum_size + group_heads :]
    joined = jnp.max(part_peaks, axis=0)
    scales = jnp.exp(part_peaks - joined[None])
    merged_totals = jnp.sum(part_totals * scales, axis=0)
    merged_sums = jnp.sum(part_sums * scales[..., None], axis=0)
    attended = (merged_sums / merged_totals[..., None]).reshape(1, H * HD)
    attended = jnp.broadcast_to(attended[None], (groups,) + attended.shape)
    attended = lax.all_to_all(attended, "grp", 0, 0, tiled=True)
    return attended.reshape(rows, H * HD)


def solution(mesh):
    groups, blocks = mesh.shape["grp"], mesh.shape["blk"]
    inner = Mesh(mesh.devices.reshape(groups, KV, blocks // KV), ("grp", "w", "zq"))
    rows = ("w", "zq")
    return jax.shard_map(
        local,
        mesh=inner,
        in_specs=(
            P(rows, None),
            P(("grp",) + rows, None),
            P(("grp",) + rows, None),
            P(("grp",) + rows, None),
            P(("grp",) + rows, None),
            P(),
        ),
        out_specs=P(rows, None),
        check_vma=False,
    )
```

```python
import functools
import math

import jax
import jax.numpy as jnp
from jax import lax
from jax.experimental import pallas as pl
from jax.experimental.pallas import tpu as pltpu
from jax.sharding import Mesh
from jax.sharding import PartitionSpec as P

H = 64
KV = 8
HD = 128


def split_product(weights, values):
    rounded = lax.reduce_precision(weights, exponent_bits=8, mantissa_bits=7)
    high = rounded.astype(jnp.bfloat16)
    low = (weights - rounded).astype(jnp.bfloat16)
    spec = "rgp,pd->rgd"
    return jnp.einsum(spec, high, values, preferred_element_type=jnp.float32) + jnp.einsum(
        spec, low, values, preferred_element_type=jnp.float32
    )


def attend_kernel(inverse_root, query_ref, key_ref, value_ref, sum_ref, peak_ref, total_ref):
    scores = lax.dot_general(
        query_ref[...],
        key_ref[...],
        (((1,), (1,)), ((), ())),
        preferred_element_type=jnp.float32,
    ) * inverse_root
    peak = jnp.max(scores, axis=1, keepdims=True)
    weights = jnp.exp(scores - peak)
    total_ref[...] = jnp.sum(weights, axis=1, keepdims=True)
    peak_ref[...] = peak
    high = weights.astype(jnp.bfloat16)
    low = (weights - high.astype(jnp.float32)).astype(jnp.bfloat16)
    values = value_ref[...]
    sum_ref[...] = jnp.dot(high, values, preferred_element_type=jnp.float32) + jnp.dot(
        low, values, preferred_element_type=jnp.float32
    )


def attend_prefix(query_rows, keys, values, inverse_root):
    count, width = query_rows.shape
    length = keys.shape[0]
    tile = 256
    return pl.pallas_call(
        functools.partial(attend_kernel, inverse_root),
        grid=(count // tile,),
        in_specs=[
            pl.BlockSpec((tile, width), lambda i: (i, 0)),
            pl.BlockSpec((length, width), lambda i: (0, 0)),
            pl.BlockSpec((length, width), lambda i: (0, 0)),
        ],
        out_specs=[
            pl.BlockSpec((tile, width), lambda i: (i, 0)),
            pl.BlockSpec((tile, 1), lambda i: (i, 0)),
            pl.BlockSpec((tile, 1), lambda i: (i, 0)),
        ],
        out_shape=[
            jax.ShapeDtypeStruct((count, width), jnp.float32),
            jax.ShapeDtypeStruct((count, 1), jnp.float32),
            jax.ShapeDtypeStruct((count, 1), jnp.float32),
        ],
        compiler_params=pltpu.CompilerParams(vmem_limit_bytes=48 * 1024 * 1024),
        cost_estimate=pl.CostEstimate(
            flops=6 * count * length * width,
            transcendentals=count * length,
            bytes_accessed=2 * count * width + 4 * length * width + 4 * count * (width + 2),
        ),
    )(query_rows, keys, values)


def local(queries, prefix_keys, prefix_values, draft_keys, draft_values, draft_offset):
    group_heads = H // KV
    rows = queries.shape[0]
    positions = prefix_keys.shape[0]
    ways = lax.axis_size("w")
    quarters = lax.axis_size("zq")
    quarter = lax.axis_index("zq")
    group = lax.axis_index("grp")
    inverse_root = 1.0 / math.sqrt(HD)

    query_heads = queries.reshape(rows, KV, group_heads * HD).transpose(1, 0, 2).reshape(KV, -1)
    key_heads = prefix_keys.reshape(positions, KV, HD).transpose(1, 0, 2).reshape(KV, -1)
    value_heads = prefix_values.reshape(positions, KV, HD).transpose(1, 0, 2).reshape(KV, -1)
    draft_key_heads = draft_keys.reshape(KV, HD)
    draft_value_heads = draft_values.reshape(KV, HD)
    send = jnp.concatenate(
        [query_heads, key_heads, draft_key_heads, value_heads, draft_value_heads], axis=1
    )
    got = lax.all_to_all(send, "w", 0, 0, tiled=True)

    query_size = rows * group_heads * HD
    key_size = positions * HD
    cut = [query_size, key_size, HD, key_size, HD]
    starts = [sum(cut[:n]) for n in range(len(cut))]
    query_block = got[:, : query_size].reshape(ways * rows, group_heads, HD)
    keys_here = jnp.concatenate(
        [
            got[:, starts[1] : starts[1] + key_size].reshape(ways * positions, HD),
            got[:, starts[2] : starts[2] + HD],
        ],
        axis=0,
    )
    values_here = jnp.concatenate(
        [
            got[:, starts[3] : starts[3] + key_size].reshape(ways * positions, HD),
            got[:, starts[4] : starts[4] + HD],
        ],
        axis=0,
    )
    local_keys = ways * positions
    both_here = jnp.stack([keys_here, values_here])
    def swap(value, mask):
        return lax.ppermute(value, "zq", [(i, i ^ mask) for i in range(quarters)])
    across = swap(both_here, 2)
    blocks = [both_here, swap(both_here, 1), across, swap(across, 1)]
    draft_k = jnp.concatenate([block[0, local_keys:] for block in blocks], axis=0)
    draft_v = jnp.concatenate([block[1, local_keys:] for block in blocks], axis=0)
    source_quarter = jnp.bitwise_xor(quarter, lax.iota(jnp.int32, quarters))

    block_rows = ways * rows
    query_rows = query_block.reshape(block_rows * group_heads, HD)
    pieces = [
        attend_prefix(query_rows, block[0, :local_keys], block[1, :local_keys], inverse_root)
        for block in blocks
    ]
    prefix_peak = functools.reduce(jnp.maximum, [piece[1] for piece in pieces])
    piece_scales = [jnp.exp(piece[1] - prefix_peak) for piece in pieces]
    prefix_total = sum(piece[2] * scale for piece, scale in zip(pieces, piece_scales))
    prefix_sum = sum(piece[0] * scale for piece, scale in zip(pieces, piece_scales))
    prefix_sum = prefix_sum.reshape(block_rows, group_heads, HD)
    prefix_peak = prefix_peak.reshape(block_rows, group_heads)
    prefix_total = prefix_total.reshape(block_rows, group_heads)
    scores_draft = jnp.einsum(
        "rgd,jd->rgj", query_block, draft_k, preferred_element_type=jnp.float32
    ) * inverse_root

    block_index = lax.iota(jnp.int32, block_rows)
    query_index = ((block_index // rows) * quarters + quarter) * rows + block_index % rows
    drafts_per_group = quarters * ways
    draft_source = (lax.iota(jnp.int32, ways)[None, :] * quarters + source_quarter[:, None]).reshape(-1)
    key_index = group * drafts_per_group + draft_source
    offsets = lax.dynamic_slice_in_dim(
        draft_offset.reshape(ways, quarters, rows), quarter, 1, axis=1
    ).reshape(block_rows)
    visible = (key_index[None, :] <= query_index[:, None]) & (
        key_index[None, :] >= (query_index - offsets)[:, None]
    )
    visible = visible[:, None, :]
    masked_draft = jnp.where(visible, scores_draft, -jnp.inf)
    peak = jnp.maximum(prefix_peak, jnp.max(masked_draft, axis=2))
    prefix_scale = jnp.exp(prefix_peak - peak)
    weights_draft = jnp.where(visible, jnp.exp(masked_draft - peak[..., None]), 0.0)
    totals = prefix_total * prefix_scale + jnp.sum(weights_draft, axis=2)
    summed = prefix_sum * prefix_scale[..., None] + split_product(weights_draft, draft_v)

    groups = lax.axis_size("grp")
    def by_destination(part):
        part = part.reshape((ways, groups) + part.shape[1:])
        return part.transpose((1, 0) + tuple(range(2, part.ndim))).reshape(groups * ways, -1)
    packed = jnp.concatenate(
        [by_destination(summed), by_destination(peak), by_destination(totals)], axis=1
    )
    parts = lax.all_to_all(packed, ("grp", "w"), 0, 0, tiled=True)
    sum_size = group_heads * HD
    parts = parts.reshape(groups, KV, -1)
    part_sums = parts[:, :, :sum_size].reshape(groups, KV, group_heads, HD)
    part_peaks = parts[:, :, sum_size : sum_size + group_heads]
    part_totals = parts[:, :, sum_size + group_heads :]
    joined = jnp.max(part_peaks, axis=0)
    scales = jnp.exp(part_peaks - joined[None])
    merged_totals = jnp.sum(part_totals * scales, axis=0)
    merged_sums = jnp.sum(part_sums * scales[..., None], axis=0)
    attended = (merged_sums / merged_totals[..., None]).reshape(1, H * HD)
    attended = jnp.broadcast_to(attended[None], (groups,) + attended.shape)
    attended = lax.all_to_all(attended, "grp", 0, 0, tiled=True)
    return attended.reshape(rows, H * HD)


def solution(mesh):
    groups, blocks = mesh.shape["grp"], mesh.shape["blk"]
    inner = Mesh(mesh.devices.reshape(groups, KV, blocks // KV), ("grp", "w", "zq"))
    rows = ("w", "zq")
    return jax.shard_map(
        local,
        mesh=inner,
        in_specs=(
            P(rows, None),
            P(("grp",) + rows, None),
            P(("grp",) + rows, None),
            P(("grp",) + rows, None),
            P(("grp",) + rows, None),
            P(),
        ),
        out_specs=P(rows, None),
        check_vma=False,
    )
```

```python
import functools
import math

import jax
import jax.numpy as jnp
from jax import lax
from jax.experimental import pallas as pl
from jax.experimental.pallas import tpu as pltpu
from jax.sharding import Mesh
from jax.sharding import PartitionSpec as P

H = 64
KV = 8
HD = 128


def split_product(weights, values):
    rounded = lax.reduce_precision(weights, exponent_bits=8, mantissa_bits=7)
    high = rounded.astype(jnp.bfloat16)
    low = (weights - rounded).astype(jnp.bfloat16)
    spec = "rgp,pd->rgd"
    return jnp.einsum(spec, high, values, preferred_element_type=jnp.float32) + jnp.einsum(
        spec, low, values, preferred_element_type=jnp.float32
    )


def attend_kernel(inverse_root, query_ref, key_ref, value_ref, sum_ref, peak_ref, total_ref):
    scores = lax.dot_general(
        query_ref[...],
        key_ref[...],
        (((1,), (1,)), ((), ())),
        preferred_element_type=jnp.float32,
    ) * inverse_root
    peak = jnp.max(scores, axis=1, keepdims=True)
    weights = jnp.exp(scores - peak)
    total_ref[...] = jnp.sum(weights, axis=1, keepdims=True)
    peak_ref[...] = peak
    high = weights.astype(jnp.bfloat16)
    low = (weights - high.astype(jnp.float32)).astype(jnp.bfloat16)
    values = value_ref[...]
    sum_ref[...] = jnp.dot(high, values, preferred_element_type=jnp.float32) + jnp.dot(
        low, values, preferred_element_type=jnp.float32
    )


def attend_prefix(query_rows, keys, values, inverse_root):
    count, width = query_rows.shape
    length = keys.shape[0]
    tile = 256
    return pl.pallas_call(
        functools.partial(attend_kernel, inverse_root),
        grid=(count // tile,),
        in_specs=[
            pl.BlockSpec((tile, width), lambda i: (i, 0)),
            pl.BlockSpec((length, width), lambda i: (0, 0)),
            pl.BlockSpec((length, width), lambda i: (0, 0)),
        ],
        out_specs=[
            pl.BlockSpec((tile, width), lambda i: (i, 0)),
            pl.BlockSpec((tile, 1), lambda i: (i, 0)),
            pl.BlockSpec((tile, 1), lambda i: (i, 0)),
        ],
        out_shape=[
            jax.ShapeDtypeStruct((count, width), jnp.float32),
            jax.ShapeDtypeStruct((count, 1), jnp.float32),
            jax.ShapeDtypeStruct((count, 1), jnp.float32),
        ],
        compiler_params=pltpu.CompilerParams(vmem_limit_bytes=48 * 1024 * 1024),
        cost_estimate=pl.CostEstimate(
            flops=6 * count * length * width,
            transcendentals=count * length,
            bytes_accessed=2 * count * width + 4 * length * width + 4 * count * (width + 2),
        ),
    )(query_rows, keys, values)


def local(queries, prefix_keys, prefix_values, draft_keys, draft_values, draft_offset):
    group_heads = H // KV
    rows = queries.shape[0]
    positions = prefix_keys.shape[0]
    ways = lax.axis_size("w")
    quarters = lax.axis_size("zq")
    quarter = lax.axis_index("zq")
    group = lax.axis_index("grp")
    inverse_root = 1.0 / math.sqrt(HD)

    query_heads = queries.reshape(rows, KV, group_heads * HD).transpose(1, 0, 2).reshape(KV, -1)
    key_heads = prefix_keys.reshape(positions, KV, HD).transpose(1, 0, 2).reshape(KV, -1)
    value_heads = prefix_values.reshape(positions, KV, HD).transpose(1, 0, 2).reshape(KV, -1)
    draft_key_heads = draft_keys.reshape(KV, HD)
    draft_value_heads = draft_values.reshape(KV, HD)
    send = jnp.concatenate(
        [query_heads, key_heads, draft_key_heads, value_heads, draft_value_heads], axis=1
    )
    got = lax.all_to_all(send, "w", 0, 0, tiled=True)

    query_size = rows * group_heads * HD
    key_size = positions * HD
    cut = [query_size, key_size, HD, key_size, HD]
    starts = [sum(cut[:n]) for n in range(len(cut))]
    query_block = got[:, : query_size].reshape(ways * rows, group_heads, HD)
    keys_here = jnp.concatenate(
        [
            got[:, starts[1] : starts[1] + key_size].reshape(ways * positions, HD),
            got[:, starts[2] : starts[2] + HD],
        ],
        axis=0,
    )
    values_here = jnp.concatenate(
        [
            got[:, starts[3] : starts[3] + key_size].reshape(ways * positions, HD),
            got[:, starts[4] : starts[4] + HD],
        ],
        axis=0,
    )
    local_keys = ways * positions
    both_here = jnp.stack([keys_here, values_here])
    def swap(value, mask):
        return lax.ppermute(value, "zq", [(i, i ^ mask) for i in range(quarters)])
    across = swap(both_here, 2)
    blocks = [both_here, swap(both_here, 1), across, swap(across, 1)]
    draft_k = jnp.concatenate([block[0, local_keys:] for block in blocks], axis=0)
    draft_v = jnp.concatenate([block[1, local_keys:] for block in blocks], axis=0)
    source_quarter = jnp.bitwise_xor(quarter, lax.iota(jnp.int32, quarters))

    block_rows = ways * rows
    query_rows = query_block.reshape(block_rows * group_heads, HD)
    pieces = [
        attend_prefix(query_rows, block[0, :local_keys], block[1, :local_keys], inverse_root)
        for block in blocks
    ]
    prefix_peak = functools.reduce(jnp.maximum, [piece[1] for piece in pieces])
    piece_scales = [jnp.exp(piece[1] - prefix_peak) for piece in pieces]
    prefix_total = sum(piece[2] * scale for piece, scale in zip(pieces, piece_scales))
    prefix_sum = sum(piece[0] * scale for piece, scale in zip(pieces, piece_scales))
    prefix_sum = prefix_sum.reshape(block_rows, group_heads, HD)
    prefix_peak = prefix_peak.reshape(block_rows, group_heads)
    prefix_total = prefix_total.reshape(block_rows, group_heads)
    scores_draft = jnp.einsum(
        "rgd,jd->rgj", query_block, draft_k, preferred_element_type=jnp.float32
    ) * inverse_root

    block_index = lax.iota(jnp.int32, block_rows)
    query_index = ((block_index // rows) * quarters + quarter) * rows + block_index % rows
    drafts_per_group = quarters * ways
    draft_source = (lax.iota(jnp.int32, ways)[None, :] * quarters + source_quarter[:, None]).reshape(-1)
    key_index = group * drafts_per_group + draft_source
    offsets = lax.dynamic_slice_in_dim(
        draft_offset.reshape(ways, quarters, rows), quarter, 1, axis=1
    ).reshape(block_rows)
    visible = (key_index[None, :] <= query_index[:, None]) & (
        key_index[None, :] >= (query_index - offsets)[:, None]
    )
    visible = visible[:, None, :]
    masked_draft = jnp.where(visible, scores_draft, -jnp.inf)
    peak = jnp.maximum(prefix_peak, jnp.max(masked_draft, axis=2))
    prefix_scale = jnp.exp(prefix_peak - peak)
    weights_draft = jnp.where(visible, jnp.exp(masked_draft - peak[..., None]), 0.0)
    totals = prefix_total * prefix_scale + jnp.sum(weights_draft, axis=2)
    summed = prefix_sum * prefix_scale[..., None] + split_product(weights_draft, draft_v)

    groups = lax.axis_size("grp")
    def by_destination(part):
        return part.reshape(ways * groups, -1)
    packed = jnp.concatenate(
        [by_destination(summed), by_destination(peak), by_destination(totals)], axis=1
    )
    parts = lax.all_to_all(packed, ("w", "grp"), 0, 0, tiled=True)
    sum_size = group_heads * HD
    parts = parts.reshape(KV, groups, -1)
    part_sums = parts[:, :, :sum_size].reshape(KV, groups, group_heads, HD)
    part_peaks = parts[:, :, sum_size : sum_size + group_heads]
    part_totals = parts[:, :, sum_size + group_heads :]
    joined = jnp.max(part_peaks, axis=1)
    scales = jnp.exp(part_peaks - joined[:, None])
    merged_totals = jnp.sum(part_totals * scales, axis=1)
    merged_sums = jnp.sum(part_sums * scales[..., None], axis=1)
    attended = (merged_sums / merged_totals[..., None]).reshape(1, H * HD)
    attended = jnp.broadcast_to(attended[None], (groups,) + attended.shape)
    attended = lax.all_to_all(attended, "grp", 0, 0, tiled=True)
    return attended.reshape(rows, H * HD)


def solution(mesh):
    groups, blocks = mesh.shape["grp"], mesh.shape["blk"]
    inner = Mesh(mesh.devices.reshape(groups, KV, blocks // KV), ("grp", "w", "zq"))
    rows = ("w", "zq")
    return jax.shard_map(
        local,
        mesh=inner,
        in_specs=(
            P(rows, None),
            P(("grp",) + rows, None),
            P(("grp",) + rows, None),
            P(("grp",) + rows, None),
            P(("grp",) + rows, None),
            P(),
        ),
        out_specs=P(rows, None),
        check_vma=False,
    )
```

```python
import functools
import math

import jax
import jax.numpy as jnp
from jax import lax
from jax.experimental import pallas as pl
from jax.experimental.pallas import tpu as pltpu
from jax.sharding import Mesh
from jax.sharding import PartitionSpec as P

H = 64
KV = 8
HD = 128


def split_product(weights, values):
    rounded = lax.reduce_precision(weights, exponent_bits=8, mantissa_bits=7)
    high = rounded.astype(jnp.bfloat16)
    low = (weights - rounded).astype(jnp.bfloat16)
    spec = "rgp,pd->rgd"
    return jnp.einsum(spec, high, values, preferred_element_type=jnp.float32) + jnp.einsum(
        spec, low, values, preferred_element_type=jnp.float32
    )


def attend_kernel(
    inverse_root, query_ref, key_ref, value_ref, sum_in, peak_in, total_in, sum_ref, peak_ref, total_ref
):
    scores = lax.dot_general(
        query_ref[...],
        key_ref[...],
        (((1,), (1,)), ((), ())),
        preferred_element_type=jnp.float32,
    ) * inverse_root
    old_peak = peak_in[...]
    peak = jnp.maximum(old_peak, jnp.max(scores, axis=1, keepdims=True))
    scale = jnp.exp(old_peak - peak)
    weights = jnp.exp(scores - peak)
    total_ref[...] = total_in[...] * scale + jnp.sum(weights, axis=1, keepdims=True)
    peak_ref[...] = peak
    high = weights.astype(jnp.bfloat16)
    low = (weights - high.astype(jnp.float32)).astype(jnp.bfloat16)
    values = value_ref[...]
    sum_ref[...] = sum_in[...] * scale + (
        jnp.dot(high, values, preferred_element_type=jnp.float32)
        + jnp.dot(low, values, preferred_element_type=jnp.float32)
    )


def attend_prefix(query_rows, keys, values, inverse_root, state):
    count, width = query_rows.shape
    length = keys.shape[0]
    tile = 256
    row_block = pl.BlockSpec((tile, width), lambda i: (i, 0))
    column_block = pl.BlockSpec((tile, 1), lambda i: (i, 0))
    whole = pl.BlockSpec((length, width), lambda i: (0, 0))
    return pl.pallas_call(
        functools.partial(attend_kernel, inverse_root),
        grid=(count // tile,),
        in_specs=[row_block, whole, whole, row_block, column_block, column_block],
        out_specs=[row_block, column_block, column_block],
        out_shape=[
            jax.ShapeDtypeStruct((count, width), jnp.float32),
            jax.ShapeDtypeStruct((count, 1), jnp.float32),
            jax.ShapeDtypeStruct((count, 1), jnp.float32),
        ],
        input_output_aliases={3: 0, 4: 1, 5: 2},
        compiler_params=pltpu.CompilerParams(vmem_limit_bytes=48 * 1024 * 1024),
        cost_estimate=pl.CostEstimate(
            flops=6 * count * length * width,
            transcendentals=count * length,
            bytes_accessed=2 * count * width + 4 * length * width + 8 * count * (width + 2),
        ),
    )(query_rows, keys, values, *state)


def local(queries, prefix_keys, prefix_values, draft_keys, draft_values, draft_offset):
    group_heads = H // KV
    rows = queries.shape[0]
    positions = prefix_keys.shape[0]
    ways = lax.axis_size("w")
    quarters = lax.axis_size("zq")
    quarter = lax.axis_index("zq")
    group = lax.axis_index("grp")
    inverse_root = 1.0 / math.sqrt(HD)

    query_heads = queries.reshape(rows, KV, group_heads * HD).transpose(1, 0, 2).reshape(KV, -1)
    key_heads = prefix_keys.reshape(positions, KV, HD).transpose(1, 0, 2).reshape(KV, -1)
    value_heads = prefix_values.reshape(positions, KV, HD).transpose(1, 0, 2).reshape(KV, -1)
    draft_key_heads = draft_keys.reshape(KV, HD)
    draft_value_heads = draft_values.reshape(KV, HD)
    send = jnp.concatenate(
        [query_heads, key_heads, draft_key_heads, value_heads, draft_value_heads], axis=1
    )
    got = lax.all_to_all(send, "w", 0, 0, tiled=True)

    query_size = rows * group_heads * HD
    key_size = positions * HD
    cut = [query_size, key_size, HD, key_size, HD]
    starts = [sum(cut[:n]) for n in range(len(cut))]
    query_block = got[:, : query_size].reshape(ways * rows, group_heads, HD)
    keys_here = jnp.concatenate(
        [
            got[:, starts[1] : starts[1] + key_size].reshape(ways * positions, HD),
            got[:, starts[2] : starts[2] + HD],
        ],
        axis=0,
    )
    values_here = jnp.concatenate(
        [
            got[:, starts[3] : starts[3] + key_size].reshape(ways * positions, HD),
            got[:, starts[4] : starts[4] + HD],
        ],
        axis=0,
    )
    local_keys = ways * positions
    both_here = jnp.stack([keys_here, values_here])
    def swap(value, mask):
        return lax.ppermute(value, "zq", [(i, i ^ mask) for i in range(quarters)])
    across = swap(both_here, 2)
    blocks = [both_here, swap(both_here, 1), across, swap(across, 1)]
    draft_k = jnp.concatenate([block[0, local_keys:] for block in blocks], axis=0)
    draft_v = jnp.concatenate([block[1, local_keys:] for block in blocks], axis=0)
    source_quarter = jnp.bitwise_xor(quarter, lax.iota(jnp.int32, quarters))

    block_rows = ways * rows
    query_rows = query_block.reshape(block_rows * group_heads, HD)
    rows_total = block_rows * group_heads
    state = (
        jnp.zeros((rows_total, HD), jnp.float32),
        jnp.full((rows_total, 1), -jnp.inf, jnp.float32),
        jnp.zeros((rows_total, 1), jnp.float32),
    )
    for block in blocks:
        state = attend_prefix(query_rows, block[0, :local_keys], block[1, :local_keys], inverse_root, state)
    prefix_sum, prefix_peak, prefix_total = state
    prefix_sum = prefix_sum.reshape(block_rows, group_heads, HD)
    prefix_peak = prefix_peak.reshape(block_rows, group_heads)
    prefix_total = prefix_total.reshape(block_rows, group_heads)
    scores_draft = jnp.einsum(
        "rgd,jd->rgj", query_block, draft_k, preferred_element_type=jnp.float32
    ) * inverse_root

    block_index = lax.iota(jnp.int32, block_rows)
    query_index = ((block_index // rows) * quarters + quarter) * rows + block_index % rows
    drafts_per_group = quarters * ways
    draft_source = (lax.iota(jnp.int32, ways)[None, :] * quarters + source_quarter[:, None]).reshape(-1)
    key_index = group * drafts_per_group + draft_source
    offsets = lax.dynamic_slice_in_dim(
        draft_offset.reshape(ways, quarters, rows), quarter, 1, axis=1
    ).reshape(block_rows)
    visible = (key_index[None, :] <= query_index[:, None]) & (
        key_index[None, :] >= (query_index - offsets)[:, None]
    )
    visible = visible[:, None, :]
    masked_draft = jnp.where(visible, scores_draft, -jnp.inf)
    peak = jnp.maximum(prefix_peak, jnp.max(masked_draft, axis=2))
    prefix_scale = jnp.exp(prefix_peak - peak)
    weights_draft = jnp.where(visible, jnp.exp(masked_draft - peak[..., None]), 0.0)
    totals = prefix_total * prefix_scale + jnp.sum(weights_draft, axis=2)
    summed = prefix_sum * prefix_scale[..., None] + split_product(weights_draft, draft_v)

    groups = lax.axis_size("grp")
    def by_destination(part):
        return part.reshape(ways * groups, -1)
    packed = jnp.concatenate(
        [by_destination(summed), by_destination(peak), by_destination(totals)], axis=1
    )
    parts = lax.all_to_all(packed, ("w", "grp"), 0, 0, tiled=True)
    sum_size = group_heads * HD
    parts = parts.reshape(KV, groups, -1)
    part_sums = parts[:, :, :sum_size].reshape(KV, groups, group_heads, HD)
    part_peaks = parts[:, :, sum_size : sum_size + group_heads]
    part_totals = parts[:, :, sum_size + group_heads :]
    joined = jnp.max(part_peaks, axis=1)
    scales = jnp.exp(part_peaks - joined[:, None])
    merged_totals = jnp.sum(part_totals * scales, axis=1)
    merged_sums = jnp.sum(part_sums * scales[..., None], axis=1)
    attended = (merged_sums / merged_totals[..., None]).reshape(1, H * HD)
    attended = jnp.broadcast_to(attended[None], (groups,) + attended.shape)
    attended = lax.all_to_all(attended, "grp", 0, 0, tiled=True)
    return attended.reshape(rows, H * HD)


def solution(mesh):
    groups, blocks = mesh.shape["grp"], mesh.shape["blk"]
    inner = Mesh(mesh.devices.reshape(groups, KV, blocks // KV), ("grp", "w", "zq"))
    rows = ("w", "zq")
    return jax.shard_map(
        local,
        mesh=inner,
        in_specs=(
            P(rows, None),
            P(("grp",) + rows, None),
            P(("grp",) + rows, None),
            P(("grp",) + rows, None),
            P(("grp",) + rows, None),
            P(),
        ),
        out_specs=P(rows, None),
        check_vma=False,
    )
```
